128 devices in a mesh: seq: 32 (over y, z, core), head: 4 (over x).
Axes of the slice: x: 4, y: 4, z: 4, core: 2. Of those that a mesh axis runs over, the one named last changes fastest.
Arguments:
- queries: bfloat16 [8192, 2048], P('seq', 'head'), parts along dimension 1, may hold values from -6 to 6
- keys: bfloat16 [8192, 512], P('seq', 'head'), parts along dimension 1, may hold values from -6 to 6
- values: bfloat16 [8192, 512], P('seq', 'head'), parts along dimension 1, may hold values from -6 to 6
- grad_out: bfloat16 [8192, 2048], P('seq', 'head'), parts along dimension 1, may hold values from -6 to 6
- lengths: int32 [16], replicated, may hold values from 1 to 2048, 8192 in all
- send_order: int32 [32, 256], replicated, may hold values from 0 to 255, each once within a row
Outputs:
- attended: float32 [8192, 2048], P('seq', 'head'), parts along dimension 1
- grad_queries: float32 [8192, 2048], P('seq', 'head'), parts along dimension 1
- grad_keys: float32 [8192, 512], P('seq', 'head'), parts along dimension 1
- grad_values: float32 [8192, 512], P('seq', 'head'), parts along dimension 1
The draws below stay inside these ranges and needn't reach their ends.
There are 4 independent parts, one for each index of `head`. The reference program is written for one: setup_inputs(seed, part) draws one part's arguments, and reference() takes and returns one part's arrays. A program takes and returns all parts, laid end to end along the dimension named above; an argument that names none is the same for every part. Nothing has to cross between parts.
Inputs may be any that keep to these rules, and one draw needn't show every extreme that they name: `lengths`: they sum to 8192; the longest is exactly 2048. `send_order`: each row is a permutation of 0 to 255.
All inputs are finite; a program needn't handle non-finite values.
Results may differ from the reference program's by a relative error of at most 0.039.
Values may be sent and summed in bfloat16 or wider, within the bound.
No kernel may reach another device: no remote copies, remote signals or barrier semaphores. Data moves between devices by JAX's collectives and lax.ppermute only.
A program may use at most 64 MiB of HBM per device.

```python
import math
import jax
import jax.numpy as jnp
import numpy as np
from jax import lax

HD = 128
QH = 4
TOK_DEV = 256
DOCS = 16
SHARDS = 32
GROUP = 8
TOKENS = 8192
LONGEST = 2048


def draw_queries(key, part):
    base = jnp.clip(1.5 * jax.random.normal(jax.random.fold_in(key, 1), (TOKENS, QH, HD), jnp.float32), -6.0, 6.0)
    return base.reshape(TOKENS, QH * HD).astype(jnp.bfloat16)


def draw_keys(key, part):
    base = jnp.clip(jax.random.normal(jax.random.fold_in(key, 2), (TOKENS, HD), jnp.float32), -6.0, 6.0)
    return base.astype(jnp.bfloat16)


def draw_values(key, part):
    base = jnp.clip(jax.random.normal(jax.random.fold_in(key, 3), (TOKENS, HD), jnp.float32), -6.0, 6.0)
    return base.astype(jnp.bfloat16)


def block_scale(stream_key, extent, pieces, smallest, high):
    factor_of, own = 1.0, jax.random.fold_in(stream_key, 6)
    for dim, blocks in pieces:
        draws = jnp.exp(jax.random.uniform(jax.random.fold_in(own, dim), (blocks,), jnp.float32, smallest / len(pieces), high / len(pieces)))
        factor_of = factor_of * jnp.repeat(draws, extent[dim] // blocks).reshape([-1 if axis == dim else 1 for axis in range(len(extent))])
    return factor_of


def profile(count, total, limit, slope):
    portions = [(1 << 20) // math.isqrt(rank ** slope) + 1 for rank in range(2, count + 1)]
    rest, counts = total - limit - (count - 1), [1] * (count - 1)
    while rest > 0:
        movable = [i for i in range(count - 1) if counts[i] < limit]
        whole, remaining = sum([portions[i] for i in movable]), rest
        for i in movable:
            extra = min(limit - counts[i], max(1, remaining * portions[i] // whole), rest)
            counts[i] = counts[i] + extra
            rest = rest - extra
    return np.array([limit] + counts)


def ragged(rng, number_of, total, bound, lean):
    if number_of == 2:
        one = jax.random.randint(rng, (), max(1, total - bound), min(bound, total - 1) + 1)
        return jnp.stack([one, total - one])
    sizes = jnp.asarray(profile(number_of, total, bound, lean), jnp.int32)
    couples = (number_of - 1) // 2
    giver, taker = sizes[1:1 + 2 * couples:2], sizes[2:2 + 2 * couples:2]
    slack = jnp.minimum(giver - 1, bound - taker)
    moved = jax.random.randint(jax.random.fold_in(rng, 1), (couples,), 0, 1 << 20) % (slack + 1)
    sizes = sizes.at[1:1 + 2 * couples:2].set(giver - moved).at[2:2 + 2 * couples:2].set(taker + moved)
    return sizes[jax.random.permutation(jax.random.fold_in(rng, 2), number_of)]


def gaussian(stream_key, dims, deviation, limit, split=(), held_as=jnp.bfloat16):
    entries = jax.random.normal(stream_key, dims, jnp.float32) * deviation
    if len(split) > 0:
        entries = block_scale(stream_key, dims, split, -0.22, 0.18) * entries
    return jnp.clip(entries, min=-limit, max=limit).astype(held_as)


def setup_inputs(seed: int = 0, part: int = 0) -> dict:
    key_list = jax.random.split(jax.random.key(seed), 7)
    part_splits = jax.random.split(jax.random.fold_in(key_list[6], part), 7)
    return {
        "queries": draw_queries(jax.random.fold_in(jax.random.fold_in(key_list[6], part), 71), part),
        "keys": draw_keys(jax.random.fold_in(jax.random.fold_in(key_list[6], part), 71), part),
        "values": draw_values(jax.random.fold_in(jax.random.fold_in(key_list[6], part), 71), part),
        "grad_out": gaussian(part_splits[3], (TOKENS, QH * HD), 1.0, 6.0, ((0, 32),)),
        "lengths": ragged(key_list[4], DOCS, TOKENS, LONGEST, 2).astype(jnp.int32),
        "send_order": jax.vmap(lambda own: jax.random.permutation(own, TOK_DEV))(jax.random.split(key_list[5], SHARDS)).reshape((SHARDS, TOK_DEV)).astype(jnp.int32),
    }


masked_value = -1e+30

def doc_index(positions, bounds):
    return lax.optimization_barrier(jnp.sum((positions[:, None] >= bounds[None, :]).astype(jnp.int32), axis=1))

def reference(queries, keys, values, grad_out, lengths, send_order):
    bounds = jnp.cumsum(lengths)
    order_blocks = send_order.reshape(SHARDS, SHARDS, GROUP).transpose(1, 0, 2)
    source = (jnp.arange(SHARDS, dtype=jnp.int32)[None, :, None] * TOK_DEV + order_blocks).reshape(TOKENS).astype(jnp.int32)
    picked = jnp.take(queries, source, axis=0).reshape(TOKENS, QH, HD)
    grad_heads = grad_out.reshape(TOKENS, QH, HD)
    key_pos = jnp.arange(TOKENS, dtype=jnp.int32)
    key_doc = doc_index(key_pos, bounds)
    key_float = keys.astype(jnp.float32)
    value_float = values.astype(jnp.float32)
    score_scale = 1.0 / math.sqrt(HD)
    block_rows = math.gcd(TOKENS, 512)
    block_count = TOKENS // block_rows

    def query_block(sums, block_item):
        query_heads, grad_block, query_pos = block_item
        query_doc = doc_index(query_pos, bounds)
        allowed = ((query_doc[:, None] == key_doc[None, :]) & (key_pos[None, :] <= query_pos[:, None]))[:, None, :]
        query_float = query_heads.astype(jnp.float32)
        grad_float = grad_block.astype(jnp.float32)
        scores = jnp.where(allowed, jnp.einsum('bhd,td->bht', query_float, key_float) * score_scale, masked_value)
        row_max = lax.optimization_barrier(jnp.max(scores, axis=2))
        log_total = row_max + jnp.log(lax.optimization_barrier(jnp.sum(jnp.exp(scores - row_max[:, :, None]), axis=2)))
        weights = jnp.where(allowed, jnp.exp(scores - log_total[:, :, None]), 0.0)
        weights_low = weights.astype(jnp.bfloat16)
        attended = jnp.einsum('bht,td->bhd', weights, value_float)
        attended_low = attended.astype(jnp.bfloat16)
        out_dot = lax.optimization_barrier(jnp.sum(grad_float * attended_low.astype(jnp.float32), axis=2))
        grad_dots = jnp.einsum('bhd,td->bht', grad_float, value_float)
        score_grads = (weights * (grad_dots - out_dot[:, :, None])).astype(jnp.bfloat16)
        grads_float = score_grads.astype(jnp.float32)
        grad_query = jnp.einsum('bht,td->bhd', grads_float, key_float) * score_scale
        key_sums = sums[0] + jnp.einsum('bht,bhd->td', grads_float, query_float) * score_scale
        value_sums = sums[1] + jnp.einsum('bht,bhd->td', weights_low.astype(jnp.float32), grad_float)
        return ((key_sums, value_sums), (attended, grad_query))
    zero_sums = (jnp.zeros((TOKENS, HD), jnp.float32), jnp.zeros((TOKENS, HD), jnp.float32))
    block_items = (picked.reshape(block_count, block_rows, QH, HD), grad_heads.reshape(block_count, block_rows, QH, HD), source.reshape(block_count, block_rows))
    (key_sums, value_sums), (attended, grad_query) = lax.scan(query_block, zero_sums, block_items)
    return (attended.reshape(TOKENS, QH * HD), grad_query.reshape(TOKENS, QH * HD), key_sums, value_sums)
```

```python
import math

import jax
import jax.numpy as jnp
from jax import lax
from jax.sharding import PartitionSpec as P

masked_value = -1e30
LONGEST = 2048


def doc_index(positions, bounds):
    return jnp.sum((positions[:, None] >= bounds[None, :]).astype(jnp.int32), axis=1)


def per_device(queries, keys, values, grad_out, lengths, send_order):
    shard_count = lax.axis_size("seq")
    my_index = lax.axis_index("seq")
    tok_rows, head_dim = keys.shape
    head_count = queries.shape[1] // head_dim
    score_scale = 1.0 / math.sqrt(head_dim)
    halo = min(shard_count - 1, (LONGEST - 1 + tok_rows - 1) // tok_rows)
    bounds = jnp.cumsum(lengths)

    own_order = lax.dynamic_index_in_dim(send_order, my_index, 0, keepdims=False)
    query_rows = jnp.take(queries, own_order, axis=0)
    query_heads = query_rows.reshape(tok_rows, head_count, head_dim)
    query_pos = my_index * tok_rows + own_order
    query_doc = doc_index(query_pos, bounds)
    grad_rows = lax.all_to_all(grad_out, "seq", 0, 0, tiled=True)
    grad_heads = grad_rows.reshape(tok_rows, head_count, head_dim)

    pair = jnp.concatenate([keys, values], axis=1)
    blocks = [pair]
    for shift in range(1, halo + 1):
        blocks.append(
            lax.ppermute(pair, "seq", [(i, i + shift) for i in range(shard_count - shift)])
        )
    halo_pair = jnp.concatenate(blocks, axis=0)
    key_all = halo_pair[:, :head_dim]
    value_all = halo_pair[:, head_dim:]
    block_ids = jnp.repeat(jnp.arange(halo + 1, dtype=jnp.int32), tok_rows)
    key_pos = (my_index - block_ids) * tok_rows + jnp.tile(
        jnp.arange(tok_rows, dtype=jnp.int32), halo + 1
    )
    key_doc = doc_index(key_pos, bounds)
    allowed = (
        (query_doc[:, None] == key_doc[None, :])
        & (key_pos[None, :] <= query_pos[:, None])
        & (key_pos[None, :] >= 0)
    )[:, None, :]

    products = (
        jnp.einsum("bhd,td->bht", query_heads, key_all, preferred_element_type=jnp.float32)
        * score_scale
    )
    scores = jnp.where(allowed, products, masked_value)
    row_max = jnp.max(scores, axis=2)
    log_total = row_max + jnp.log(jnp.sum(jnp.exp(scores - row_max[:, :, None]), axis=2))
    weights = jnp.where(allowed, jnp.exp(scores - log_total[:, :, None]), 0.0)
    weights_low = weights.astype(jnp.bfloat16)
    attended = jnp.einsum(
        "bht,td->bhd", weights_low, value_all, preferred_element_type=jnp.float32
    )
    attended_low = attended.astype(jnp.bfloat16)
    out_dot = jnp.sum(grad_heads.astype(jnp.float32) * attended_low.astype(jnp.float32), axis=2)
    grad_dots = jnp.einsum(
        "bhd,td->bht", grad_heads, value_all, preferred_element_type=jnp.float32
    )
    score_grads = (weights * (grad_dots - out_dot[:, :, None])).astype(jnp.bfloat16)
    grad_query = (
        jnp.einsum("bht,td->bhd", score_grads, key_all, preferred_element_type=jnp.float32)
        * score_scale
    )
    key_term = (
        jnp.einsum("bht,bhd->td", score_grads, query_heads, preferred_element_type=jnp.float32)
        * score_scale
    )
    value_term = jnp.einsum(
        "bht,bhd->td", weights_low, grad_heads, preferred_element_type=jnp.float32
    )
    terms = jnp.concatenate([key_term, value_term], axis=1).reshape(halo + 1, tok_rows, -1)
    total = terms[0]
    for shift in range(1, halo + 1):
        total = total + lax.ppermute(
            terms[shift], "seq", [(i, i - shift) for i in range(shift, shard_count)]
        )
    key_grad = total[:, :head_dim]
    value_grad = total[:, head_dim:]

    row_outs = jnp.concatenate(
        [
            attended.reshape(tok_rows, head_count * head_dim),
            grad_query.reshape(tok_rows, head_count * head_dim),
        ],
        axis=1,
    )
    balanced = lax.all_to_all(row_outs, "seq", 0, 0, tiled=True)
    width = head_count * head_dim
    return (balanced[:, :width], balanced[:, width:], key_grad, value_grad)


def solution(mesh):
    placed = (P("seq", "head"), P("seq", "head"), P("seq", "head"), P("seq", "head"), P(), P())
    return jax.shard_map(
        per_device,
        mesh=mesh,
        in_specs=placed,
        out_specs=(P("seq", "head"), P("seq", "head"), P("seq", "head"), P("seq", "head")),
        check_vma=False,
    )
```

```python
import math

import jax
import jax.numpy as jnp
from jax import lax
from jax.sharding import PartitionSpec as P

masked_value = -1e30
LONGEST = 2048


def doc_index(positions, bounds):
    return jnp.sum((positions[:, None] >= bounds[None, :]).astype(jnp.int32), axis=1)


def per_device(queries, keys, values, grad_out, lengths, send_order):
    shard_count = lax.axis_size("seq")
    my_index = lax.axis_index("seq")
    tok_rows, head_dim = keys.shape
    head_count = queries.shape[1] // head_dim
    score_scale = 1.0 / math.sqrt(head_dim)
    halo = min(shard_count - 1, (LONGEST - 1 + tok_rows - 1) // tok_rows)
    bounds = jnp.cumsum(lengths)

    own_order = lax.dynamic_index_in_dim(send_order, my_index, 0, keepdims=False)
    query_rows = jnp.take(queries, own_order, axis=0)
    query_heads = query_rows.reshape(tok_rows, head_count, head_dim)
    query_pos = my_index * tok_rows + own_order
    query_doc = doc_index(query_pos, bounds)
    grad_rows = lax.all_to_all(grad_out, "seq", 0, 0, tiled=True)
    grad_heads = grad_rows.reshape(tok_rows, head_count, head_dim)

    pair = jnp.concatenate([keys, values], axis=1)
    blocks = [pair]
    for shift in range(1, halo + 1):
        blocks.append(
            lax.ppermute(pair, "seq", [(i, i + shift) for i in range(shard_count - shift)])
        )
    halo_pair = jnp.concatenate(blocks, axis=0)
    key_all = halo_pair[:, :head_dim]
    value_all = halo_pair[:, head_dim:]
    block_ids = jnp.repeat(jnp.arange(halo + 1, dtype=jnp.int32), tok_rows)
    key_pos = (my_index - block_ids) * tok_rows + jnp.tile(
        jnp.arange(tok_rows, dtype=jnp.int32), halo + 1
    )
    key_doc = doc_index(key_pos, bounds)
    allowed = (
        (query_doc[:, None] == key_doc[None, :])
        & (key_pos[None, :] <= query_pos[:, None])
        & (key_pos[None, :] >= 0)
    )[:, None, :]

    products = (
        jnp.einsum("bhd,td->bht", query_heads, key_all, preferred_element_type=jnp.float32)
        * score_scale
    )
    scores = jnp.where(allowed, products, masked_value)
    row_max = jnp.max(scores, axis=2)
    log_total = row_max + jnp.log(jnp.sum(jnp.exp(scores - row_max[:, :, None]), axis=2))
    weights = jnp.where(allowed, jnp.exp(scores - log_total[:, :, None]), 0.0)
    weights_low = weights.astype(jnp.bfloat16)
    attended = jnp.einsum(
        "bht,td->bhd", weights_low, value_all, preferred_element_type=jnp.float32
    )
    attended_low = attended.astype(jnp.bfloat16)
    out_dot = jnp.sum(grad_heads.astype(jnp.float32) * attended_low.astype(jnp.float32), axis=2)
    grad_dots = jnp.einsum(
        "bhd,td->bht", grad_heads, value_all, preferred_element_type=jnp.float32
    )
    score_grads = (weights * (grad_dots - out_dot[:, :, None])).astype(jnp.bfloat16)
    grad_query = (
        jnp.einsum("bht,td->bhd", score_grads, key_all, preferred_element_type=jnp.float32)
        * score_scale
    )
    width = head_count * head_dim
    attended_out = lax.all_to_all(
        attended.reshape(tok_rows, width), "seq", 0, 0, tiled=True
    )

    def block_terms(shift):
        cols = slice(shift * tok_rows, (shift + 1) * tok_rows)
        key_term = (
            jnp.einsum(
                "bht,bhd->td",
                score_grads[:, :, cols],
                query_heads,
                preferred_element_type=jnp.float32,
            )
            * score_scale
        )
        value_term = jnp.einsum(
            "bht,bhd->td", weights_low[:, :, cols], grad_heads, preferred_element_type=jnp.float32
        )
        return jnp.concatenate([key_term, value_term], axis=1)

    arrived = []
    for shift in range(halo, 0, -1):
        sent = block_terms(shift).astype(jnp.bfloat16)
        arrived.append(
            lax.ppermute(sent, "seq", [(i, i - shift) for i in range(shift, shard_count)])
        )
    total = block_terms(0)
    for part in arrived:
        total = total + part.astype(jnp.float32)
    key_grad = total[:, :head_dim]
    value_grad = total[:, head_dim:]
    query_out = lax.all_to_all(grad_query.reshape(tok_rows, width), "seq", 0, 0, tiled=True)
    return (attended_out, query_out, key_grad, value_grad)


def solution(mesh):
    placed = (P("seq", "head"), P("seq", "head"), P("seq", "head"), P("seq", "head"), P(), P())
    return jax.shard_map(
        per_device,
        mesh=mesh,
        in_specs=placed,
        out_specs=(P("seq", "head"), P("seq", "head"), P("seq", "head"), P("seq", "head")),
        check_vma=False,
    )
```

```python
import math

import jax
import jax.numpy as jnp
from jax import lax
from jax.sharding import PartitionSpec as P


masked_value = -1e30
LONGEST = 2048


def doc_index(positions, bounds):
    return jnp.sum((positions[:, None] >= bounds[None, :]).astype(jnp.int32), axis=1)


def per_device(queries, keys, values, grad_out, lengths, send_order):
    shard_count = lax.axis_size("seq")
    my_index = lax.axis_index("seq")
    tok_rows, head_dim = keys.shape
    head_count = queries.shape[1] // head_dim
    score_scale = 1.0 / math.sqrt(head_dim)
    halo = min(shard_count - 1, (LONGEST - 1 + tok_rows - 1) // tok_rows)
    bounds = jnp.cumsum(lengths)

    own_order = lax.dynamic_index_in_dim(send_order, my_index, 0, keepdims=False)
    query_rows = jnp.take(queries, own_order, axis=0)
    query_heads = query_rows.reshape(tok_rows, head_count, head_dim)
    query_pos = my_index * tok_rows + own_order
    query_doc = doc_index(query_pos, bounds)
    grad_rows = lax.all_to_all(grad_out, "seq", 0, 0, tiled=True)
    grad_heads = grad_rows.reshape(tok_rows, head_count, head_dim)

    pair = jnp.concatenate([keys, values], axis=1)
    blocks = [pair]
    for shift in range(1, halo + 1):
        blocks.append(
            lax.ppermute(pair, "seq", [(i, i + shift) for i in range(shard_count - shift)])
        )
    halo_pair = jnp.concatenate(blocks, axis=0)
    key_all = halo_pair[:, :head_dim]
    value_all = halo_pair[:, head_dim:]
    block_ids = jnp.repeat(jnp.arange(halo + 1, dtype=jnp.int32), tok_rows)
    key_pos = (my_index - block_ids) * tok_rows + jnp.tile(
        jnp.arange(tok_rows, dtype=jnp.int32), halo + 1
    )
    key_doc = doc_index(key_pos, bounds)
    allowed = (
        (query_doc[:, None] == key_doc[None, :])
        & (key_pos[None, :] <= query_pos[:, None])
        & (key_pos[None, :] >= 0)
    )[:, None, :]

    products = (
        jnp.einsum("bhd,td->bht", query_heads, key_all, preferred_element_type=jnp.float32)
        * score_scale
    )
    scores = jnp.where(allowed, products, masked_value)
    row_max = jnp.max(scores, axis=2)
    log_total = row_max + jnp.log(jnp.sum(jnp.exp(scores - row_max[:, :, None]), axis=2))
    weights = jnp.where(allowed, jnp.exp(scores - log_total[:, :, None]), 0.0)
    weights_low = weights.astype(jnp.bfloat16)
    attended = jnp.einsum(
        "bht,td->bhd", weights_low, value_all, preferred_element_type=jnp.float32
    )
    attended_low = attended.astype(jnp.bfloat16)
    out_dot = jnp.sum(grad_heads.astype(jnp.float32) * attended_low.astype(jnp.float32), axis=2)
    grad_dots = jnp.einsum(
        "bhd,td->bht", grad_heads, value_all, preferred_element_type=jnp.float32
    )
    score_grads = (weights * (grad_dots - out_dot[:, :, None])).astype(jnp.bfloat16)
    grad_query = (
        jnp.einsum("bht,td->bhd", score_grads, key_all, preferred_element_type=jnp.float32)
        * score_scale
    )
    width = head_count * head_dim

    def block_terms(shift):
        cols = slice(shift * tok_rows, (shift + 1) * tok_rows)
        key_term = (
            jnp.einsum(
                "bht,bhd->td",
                score_grads[:, :, cols],
                query_heads,
                preferred_element_type=jnp.float32,
            )
            * score_scale
        )
        value_term = jnp.einsum(
            "bht,bhd->td", weights_low[:, :, cols], grad_heads, preferred_element_type=jnp.float32
        )
        return jnp.concatenate([key_term, value_term], axis=1)

    arrived = []
    for shift in range(halo, 0, -1):
        sent = block_terms(shift).astype(jnp.bfloat16)
        arrived.append(
            lax.ppermute(sent, "seq", [(i, i - shift) for i in range(shift, shard_count)])
        )
    total = block_terms(0)
    for part in arrived:
        total = total + part.astype(jnp.float32)
    key_grad = total[:, :head_dim]
    value_grad = total[:, head_dim:]
    row_outs = jnp.concatenate(
        [attended.reshape(tok_rows, width), grad_query.reshape(tok_rows, width)], axis=1
    )
    balanced = lax.all_to_all(row_outs, "seq", 0, 0, tiled=True)
    return (balanced[:, :width], balanced[:, width:], key_grad, value_grad)


def solution(mesh):
    placed = (P("seq", "head"), P("seq", "head"), P("seq", "head"), P("seq", "head"), P(), P())
    return jax.shard_map(
        per_device,
        mesh=mesh,
        in_specs=placed,
        out_specs=(P("seq", "head"), P("seq", "head"), P("seq", "head"), P("seq", "head")),
        check_vma=False,
    )
```

```python
import math

import jax
import jax.numpy as jnp
from jax import lax
from jax.sharding import PartitionSpec as P


masked_value = -1e30
LONGEST = 2048


def doc_index(positions, bounds):
    return jnp.sum((positions[:, None] >= bounds[None, :]).astype(jnp.int32), axis=1)


def per_device(queries, keys, values, grad_out, lengths, send_order):
    shard_count = lax.axis_size("seq")
    my_index = lax.axis_index("seq")
    tok_rows, head_dim = keys.shape
    head_count = queries.shape[1] // head_dim
    score_scale = 1.0 / math.sqrt(head_dim)
    halo = min(shard_count - 1, (LONGEST - 1 + tok_rows - 1) // tok_rows)
    bounds = jnp.cumsum(lengths)

    own_order = lax.dynamic_index_in_dim(send_order, my_index, 0, keepdims=False)
    query_rows = jnp.take(queries, own_order, axis=0)
    query_heads = query_rows.reshape(tok_rows, head_count, head_dim)
    query_pos = my_index * tok_rows + own_order
    query_doc = doc_index(query_pos, bounds)
    grad_rows = lax.all_to_all(grad_out, "seq", 0, 0, tiled=True)
    grad_heads = grad_rows.reshape(tok_rows, head_count, head_dim)

    pair = jnp.concatenate([keys, values], axis=1)
    rounds = []
    covered = 1
    while covered < halo + 1:
        rounds.append((covered, min(covered, halo + 1 - covered)))
        covered += rounds[-1][1]
    blocks = [pair]
    for shift, count in rounds:
        sent = jnp.concatenate(blocks[:count], axis=0)
        got = lax.ppermute(sent, "seq", [(i, i + shift) for i in range(shard_count - shift)])
        blocks.extend(jnp.split(got, count, axis=0))
    halo_pair = jnp.concatenate(blocks, axis=0)
    key_all = halo_pair[:, :head_dim]
    value_all = halo_pair[:, head_dim:]
    block_ids = jnp.repeat(jnp.arange(halo + 1, dtype=jnp.int32), tok_rows)
    key_pos = (my_index - block_ids) * tok_rows + jnp.tile(
        jnp.arange(tok_rows, dtype=jnp.int32), halo + 1
    )
    key_doc = doc_index(key_pos, bounds)
    allowed = (
        (query_doc[:, None] == key_doc[None, :])
        & (key_pos[None, :] <= query_pos[:, None])
        & (key_pos[None, :] >= 0)
    )[:, None, :]

    products = (
        jnp.einsum("bhd,td->bht", query_heads, key_all, preferred_element_type=jnp.float32)
        * score_scale
    )
    scores = jnp.where(allowed, products, masked_value)
    row_max = jnp.max(scores, axis=2)
    log_total = row_max + jnp.log(jnp.sum(jnp.exp(scores - row_max[:, :, None]), axis=2))
    weights = jnp.where(allowed, jnp.exp(scores - log_total[:, :, None]), 0.0)
    weights_low = weights.astype(jnp.bfloat16)
    attended = jnp.einsum(
        "bht,td->bhd", weights_low, value_all, preferred_element_type=jnp.float32
    )
    attended_low = attended.astype(jnp.bfloat16)
    out_dot = jnp.sum(grad_heads.astype(jnp.float32) * attended_low.astype(jnp.float32), axis=2)
    grad_dots = jnp.einsum(
        "bhd,td->bht", grad_heads, value_all, preferred_element_type=jnp.float32
    )
    score_grads = (weights * (grad_dots - out_dot[:, :, None])).astype(jnp.bfloat16)
    grad_query = (
        jnp.einsum("bht,td->bhd", score_grads, key_all, preferred_element_type=jnp.float32)
        * score_scale
    )
    width = head_count * head_dim
    key_term = (
        jnp.einsum("bht,bhd->td", score_grads, query_heads, preferred_element_type=jnp.float32)
        * score_scale
    )
    value_term = jnp.einsum(
        "bht,bhd->td", weights_low, grad_heads, preferred_element_type=jnp.float32
    )
    terms = jnp.concatenate([key_term, value_term], axis=1)
    parts = list(jnp.split(terms, halo + 1, axis=0))
    for shift, count in reversed(rounds):
        sent = jnp.concatenate(parts[shift:shift + count], axis=0).astype(jnp.bfloat16)
        got = lax.ppermute(sent, "seq", [(i, i - shift) for i in range(shift, shard_count)])
        got_parts = jnp.split(got.astype(jnp.float32), count, axis=0)
        for slot in range(count):
            parts[slot] = parts[slot] + got_parts[slot]
    total = parts[0]
    key_grad = total[:, :head_dim]
    value_grad = total[:, head_dim:]
    row_outs = jnp.concatenate(
        [attended.reshape(tok_rows, width), grad_query.reshape(tok_rows, width)], axis=1
    )
    balanced = lax.all_to_all(row_outs, "seq", 0, 0, tiled=True)
    return (balanced[:, :width], balanced[:, width:], key_grad, value_grad)


def solution(mesh):
    placed = (P("seq", "head"), P("seq", "head"), P("seq", "head"), P("seq", "head"), P(), P())
    return jax.shard_map(
        per_device,
        mesh=mesh,
        in_specs=placed,
        out_specs=(P("seq", "head"), P("seq", "head"), P("seq", "head"), P("seq", "head")),
        check_vma=False,
    )
```

```python
import math

import jax
import jax.numpy as jnp
from jax import lax
from jax.sharding import PartitionSpec as P


masked_value = -1e30
LONGEST = 2048


def doc_index(positions, bounds):
    return jnp.sum((positions[:, None] >= bounds[None, :]).astype(jnp.int32), axis=1)


def per_device(queries, keys, values, grad_out, lengths, send_order):
    shard_count = lax.axis_size("seq")
    my_index = lax.axis_index("seq")
    tok_rows, head_dim = keys.shape
    head_count = queries.shape[1] // head_dim
    score_scale = 1.0 / math.sqrt(head_dim)
    halo = min(shard_count - 1, (LONGEST - 1 + tok_rows - 1) // tok_rows)
    bounds = jnp.cumsum(lengths)

    own_order = lax.dynamic_index_in_dim(send_order, my_index, 0, keepdims=False)
    query_rows = jnp.take(queries, own_order, axis=0)
    query_heads = query_rows.reshape(tok_rows, head_count, head_dim)
    query_pos = my_index * tok_rows + own_order
    query_doc = doc_index(query_pos, bounds)
    grad_rows = lax.all_to_all(grad_out, "seq", 0, 0, tiled=True)
    grad_heads = grad_rows.reshape(tok_rows, head_count, head_dim)

    pair = jnp.concatenate([keys, values], axis=1)
    rounds = []
    covered = 1
    while covered < halo + 1:
        rounds.append((covered, min(covered, halo + 1 - covered)))
        covered += rounds[-1][1]
    blocks = [pair]
    stages = [(0, 1)]
    for shift, count in rounds:
        sent = jnp.concatenate(blocks[:count], axis=0)
        got = lax.ppermute(sent, "seq", [(i, i + shift) for i in range(shard_count - shift)])
        stages.append((len(blocks), len(blocks) + count))
        blocks.extend(jnp.split(got, count, axis=0))

    run_max = jnp.full((tok_rows, head_count), masked_value, jnp.float32)
    run_total = jnp.zeros((tok_rows, head_count), jnp.float32)
    weighted = jnp.zeros((tok_rows, head_count, head_dim), jnp.float32)
    stage_scores = []
    stage_allowed = []
    for lo, hi in stages:
        stage_pair = jnp.concatenate(blocks[lo:hi], axis=0)
        stage_keys = stage_pair[:, :head_dim]
        stage_values = stage_pair[:, head_dim:]
        block_ids = jnp.repeat(jnp.arange(lo, hi, dtype=jnp.int32), tok_rows)
        key_pos = (my_index - block_ids) * tok_rows + jnp.tile(
            jnp.arange(tok_rows, dtype=jnp.int32), hi - lo
        )
        key_doc = doc_index(key_pos, bounds)
        allowed = (
            (query_doc[:, None] == key_doc[None, :])
            & (key_pos[None, :] <= query_pos[:, None])
            & (key_pos[None, :] >= 0)
        )[:, None, :]
        products = (
            jnp.einsum(
                "bhd,td->bht", query_heads, stage_keys, preferred_element_type=jnp.float32
            )
            * score_scale
        )
        scores = jnp.where(allowed, products, masked_value)
        new_max = jnp.maximum(run_max, jnp.max(scores, axis=2))
        exp_weights = jnp.where(allowed, jnp.exp(scores - new_max[:, :, None]), 0.0)
        rescale = jnp.exp(run_max - new_max)
        run_total = run_total * rescale + jnp.sum(exp_weights, axis=2)
        weighted = weighted * rescale[:, :, None] + jnp.einsum(
            "bht,td->bhd",
            exp_weights.astype(jnp.bfloat16),
            stage_values,
            preferred_element_type=jnp.float32,
        )
        run_max = new_max
        stage_scores.append(scores)
        stage_allowed.append(allowed)
    attended = weighted / run_total[:, :, None]
    log_total = run_max + jnp.log(run_total)

    halo_pair = jnp.concatenate(blocks, axis=0)
    key_all = halo_pair[:, :head_dim]
    value_all = halo_pair[:, head_dim:]
    scores = jnp.concatenate(stage_scores, axis=2)
    allowed = jnp.concatenate(stage_allowed, axis=2)
    weights = jnp.where(allowed, jnp.exp(scores - log_total[:, :, None]), 0.0)
    weights_low = weights.astype(jnp.bfloat16)
    attended_low = attended.astype(jnp.bfloat16)
    out_dot = jnp.sum(grad_heads.astype(jnp.float32) * attended_low.astype(jnp.float32), axis=2)
    grad_dots = jnp.einsum(
        "bhd,td->bht", grad_heads, value_all, preferred_element_type=jnp.float32
    )
    score_grads = (weights * (grad_dots - out_dot[:, :, None])).astype(jnp.bfloat16)
    grad_query = (
        jnp.einsum("bht,td->bhd", score_grads, key_all, preferred_element_type=jnp.float32)
        * score_scale
    )
    width = head_count * head_dim
    key_term = (
        jnp.einsum("bht,bhd->td", score_grads, query_heads, preferred_element_type=jnp.float32)
        * score_scale
    )
    value_term = jnp.einsum(
        "bht,bhd->td", weights_low, grad_heads, preferred_element_type=jnp.float32
    )
    terms = jnp.concatenate([key_term, value_term], axis=1)
    parts = list(jnp.split(terms, halo + 1, axis=0))
    for shift, count in reversed(rounds):
        sent = jnp.concatenate(parts[shift:shift + count], axis=0).astype(jnp.bfloat16)
        got = lax.ppermute(sent, "seq", [(i, i - shift) for i in range(shift, shard_count)])
        got_parts = jnp.split(got.astype(jnp.float32), count, axis=0)
        for slot in range(count):
            parts[slot] = parts[slot] + got_parts[slot]
    total = parts[0]
    key_grad = total[:, :head_dim]
    value_grad = total[:, head_dim:]
    row_outs = jnp.concatenate(
        [attended.reshape(tok_rows, width), grad_query.reshape(tok_rows, width)], axis=1
    )
    balanced = lax.all_to_all(row_outs, "seq", 0, 0, tiled=True)
    return (balanced[:, :width], balanced[:, width:], key_grad, value_grad)


def solution(mesh):
    placed = (P("seq", "head"), P("seq", "head"), P("seq", "head"), P("seq", "head"), P(), P())
    return jax.shard_map(
        per_device,
        mesh=mesh,
        in_specs=placed,
        out_specs=(P("seq", "head"), P("seq", "head"), P("seq", "head"), P("seq", "head")),
        check_vma=False,
    )
```

```python
import math

import jax
import jax.numpy as jnp
from jax import lax
from jax.sharding import PartitionSpec as P


masked_value = -1e30
LONGEST = 2048


def doc_index(positions, bounds):
    return jnp.sum((positions[:, None] >= bounds[None, :]).astype(jnp.int32), axis=1)


def per_device(queries, keys, values, grad_out, lengths, send_order):
    shard_count = lax.axis_size("seq")
    my_index = lax.axis_index("seq")
    tok_rows, head_dim = keys.shape
    head_count = queries.shape[1] // head_dim
    score_scale = 1.0 / math.sqrt(head_dim)
    halo = min(shard_count - 1, (LONGEST - 1 + tok_rows - 1) // tok_rows)
    bounds = jnp.cumsum(lengths)

    own_order = lax.dynamic_index_in_dim(send_order, my_index, 0, keepdims=False)
    query_rows = jnp.take(queries, own_order, axis=0)
    query_heads = query_rows.reshape(tok_rows, head_count, head_dim)
    query_pos = my_index * tok_rows + own_order
    query_doc = doc_index(query_pos, bounds)
    grad_rows = lax.all_to_all(grad_out, "seq", 0, 0, tiled=True)
    grad_heads = grad_rows.reshape(tok_rows, head_count, head_dim)

    pair = jnp.concatenate([keys, values], axis=1)
    group = math.isqrt(halo) + 1
    rounds = [
        [(shift, 1) for shift in range(1, min(group, halo + 1))],
        [
            (shift, min(group, halo + 1 - shift))
            for shift in range(group, halo + 1, group)
        ],
    ]
    blocks = [pair]
    for stage in rounds:
        arrived = []
        for shift, count in stage:
            sent = jnp.concatenate(blocks[:count], axis=0)
            got = lax.ppermute(sent, "seq", [(i, i + shift) for i in range(shard_count - shift)])
            arrived.extend(jnp.split(got, count, axis=0))
        blocks.extend(arrived)
    halo_pair = jnp.concatenate(blocks, axis=0)
    key_all = halo_pair[:, :head_dim]
    value_all = halo_pair[:, head_dim:]
    block_ids = jnp.repeat(jnp.arange(halo + 1, dtype=jnp.int32), tok_rows)
    key_pos = (my_index - block_ids) * tok_rows + jnp.tile(
        jnp.arange(tok_rows, dtype=jnp.int32), halo + 1
    )
    key_doc = doc_index(key_pos, bounds)
    allowed = (
        (query_doc[:, None] == key_doc[None, :])
        & (key_pos[None, :] <= query_pos[:, None])
        & (key_pos[None, :] >= 0)
    )[:, None, :]

    products = (
        jnp.einsum("bhd,td->bht", query_heads, key_all, preferred_element_type=jnp.float32)
        * score_scale
    )
    scores = jnp.where(allowed, products, masked_value)
    row_max = jnp.max(scores, axis=2)
    log_total = row_max + jnp.log(jnp.sum(jnp.exp(scores - row_max[:, :, None]), axis=2))
    weights = jnp.where(allowed, jnp.exp(scores - log_total[:, :, None]), 0.0)
    weights_low = weights.astype(jnp.bfloat16)
    attended = jnp.einsum(
        "bht,td->bhd", weights_low, value_all, preferred_element_type=jnp.float32
    )
    attended_low = attended.astype(jnp.bfloat16)
    out_dot = jnp.sum(grad_heads.astype(jnp.float32) * attended_low.astype(jnp.float32), axis=2)
    grad_dots = jnp.einsum(
        "bhd,td->bht", grad_heads, value_all, preferred_element_type=jnp.float32
    )
    score_grads = (weights * (grad_dots - out_dot[:, :, None])).astype(jnp.bfloat16)
    grad_query = (
        jnp.einsum("bht,td->bhd", score_grads, key_all, preferred_element_type=jnp.float32)
        * score_scale
    )
    width = head_count * head_dim
    key_term = (
        jnp.einsum("bht,bhd->td", score_grads, query_heads, preferred_element_type=jnp.float32)
        * score_scale
    )
    value_term = jnp.einsum(
        "bht,bhd->td", weights_low, grad_heads, preferred_element_type=jnp.float32
    )
    terms = jnp.concatenate([key_term, value_term], axis=1)
    parts = list(jnp.split(terms, halo + 1, axis=0))
    for stage in reversed(rounds):
        arrived = []
        for shift, count in stage:
            sent = jnp.concatenate(parts[shift:shift + count], axis=0).astype(jnp.bfloat16)
            got = lax.ppermute(sent, "seq", [(i, i - shift) for i in range(shift, shard_count)])
            arrived.append(jnp.split(got.astype(jnp.float32), count, axis=0))
        for got_parts in arrived:
            for slot, got_part in enumerate(got_parts):
                parts[slot] = parts[slot] + got_part
    total = parts[0]
    key_grad = total[:, :head_dim]
    value_grad = total[:, head_dim:]
    row_outs = jnp.concatenate(
        [attended.reshape(tok_rows, width), grad_query.reshape(tok_rows, width)], axis=1
    )
    balanced = lax.all_to_all(row_outs, "seq", 0, 0, tiled=True)
    return (balanced[:, :width], balanced[:, width:], key_grad, value_grad)


def solution(mesh):
    placed = (P("seq", "head"), P("seq", "head"), P("seq", "head"), P("seq", "head"), P(), P())
    return jax.shard_map(
        per_device,
        mesh=mesh,
        in_specs=placed,
        out_specs=(P("seq", "head"), P("seq", "head"), P("seq", "head"), P("seq", "head")),
        check_vma=False,
    )
```

```python
import math

import jax
import jax.numpy as jnp
from jax import lax
from jax.sharding import PartitionSpec as P


masked_value = -1e30
LONGEST = 2048


def doc_index(positions, bounds):
    return jnp.sum((positions[:, None] >= bounds[None, :]).astype(jnp.int32), axis=1)


def per_device(queries, keys, values, grad_out, lengths, send_order):
    shard_count = lax.axis_size("seq")
    my_index = lax.axis_index("seq")
    tok_rows, head_dim = keys.shape
    head_count = queries.shape[1] // head_dim
    score_scale = 1.0 / math.sqrt(head_dim)
    halo = min(shard_count - 1, (LONGEST - 1 + tok_rows - 1) // tok_rows)
    bounds = jnp.cumsum(lengths)

    own_order = lax.dynamic_index_in_dim(send_order, my_index, 0, keepdims=False)
    query_rows = jnp.take(queries, own_order, axis=0)
    query_heads = query_rows.reshape(tok_rows, head_count, head_dim)
    query_pos = my_index * tok_rows + own_order
    query_doc = doc_index(query_pos, bounds)
    pair = jnp.concatenate([keys, values], axis=1)
    group = math.isqrt(halo) + 1
    rounds = [
        [(shift, 1) for shift in range(1, min(group, halo + 1))],
        [
            (shift, min(group, halo + 1 - shift))
            for shift in range(group, halo + 1, group)
        ],
    ]
    blocks = [pair]
    first_round = None
    for stage in rounds:
        arrived = []
        for shift, count in stage:
            sent = jnp.concatenate(blocks[:count], axis=0)
            got = lax.ppermute(sent, "seq", [(i, i + shift) for i in range(shard_count - shift)])
            arrived.extend(jnp.split(got, count, axis=0))
        if first_round is None:
            first_round = arrived
            grad_out, _ = lax.optimization_barrier((grad_out, arrived))
        blocks.extend(arrived)
    grad_rows = lax.all_to_all(grad_out, "seq", 0, 0, tiled=True)
    grad_heads = grad_rows.reshape(tok_rows, head_count, head_dim)
    halo_pair = jnp.concatenate(blocks, axis=0)
    key_all = halo_pair[:, :head_dim]
    value_all = halo_pair[:, head_dim:]
    block_ids = jnp.repeat(jnp.arange(halo + 1, dtype=jnp.int32), tok_rows)
    key_pos = (my_index - block_ids) * tok_rows + jnp.tile(
        jnp.arange(tok_rows, dtype=jnp.int32), halo + 1
    )
    key_doc = doc_index(key_pos, bounds)
    allowed = (
        (query_doc[:, None] == key_doc[None, :])
        & (key_pos[None, :] <= query_pos[:, None])
        & (key_pos[None, :] >= 0)
    )[:, None, :]

    products = (
        jnp.einsum("bhd,td->bht", query_heads, key_all, preferred_element_type=jnp.float32)
        * score_scale
    )
    scores = jnp.where(allowed, products, masked_value)
    row_max = jnp.max(scores, axis=2)
    log_total = row_max + jnp.log(jnp.sum(jnp.exp(scores - row_max[:, :, None]), axis=2))
    weights = jnp.where(allowed, jnp.exp(scores - log_total[:, :, None]), 0.0)
    weights_low = weights.astype(jnp.bfloat16)
    attended = jnp.einsum(
        "bht,td->bhd", weights_low, value_all, preferred_element_type=jnp.float32
    )
    attended_low = attended.astype(jnp.bfloat16)
    out_dot = jnp.sum(grad_heads.astype(jnp.float32) * attended_low.astype(jnp.float32), axis=2)
    grad_dots = jnp.einsum(
        "bhd,td->bht", grad_heads, value_all, preferred_element_type=jnp.float32
    )
    score_grads = (weights * (grad_dots - out_dot[:, :, None])).astype(jnp.bfloat16)
    grad_query = (
        jnp.einsum("bht,td->bhd", score_grads, key_all, preferred_element_type=jnp.float32)
        * score_scale
    )
    width = head_count * head_dim
    key_term = (
        jnp.einsum("bht,bhd->td", score_grads, query_heads, preferred_element_type=jnp.float32)
        * score_scale
    )
    value_term = jnp.einsum(
        "bht,bhd->td", weights_low, grad_heads, preferred_element_type=jnp.float32
    )
    terms = jnp.concatenate([key_term, value_term], axis=1)
    head_part = terms[: group * tok_rows]
    first_back = None
    for stage in reversed(rounds):
        arrived = []
        for shift, count in stage:
            src_rows = head_part if shift < group else terms
            sent = src_rows[shift * tok_rows:(shift + count) * tok_rows].astype(jnp.bfloat16)
            got = lax.ppermute(
                sent, "seq", [(i, i - shift) for i in range(shift, shard_count)]
            )
            arrived.append((count, got))
        for count, got in arrived:
            head_part = head_part.at[: count * tok_rows].add(got.astype(jnp.float32))
        if first_back is None:
            first_back = head_part
    total = head_part[:tok_rows]
    key_grad = total[:, :head_dim]
    value_grad = total[:, head_dim:]
    row_outs = jnp.concatenate(
        [attended.reshape(tok_rows, width), grad_query.reshape(tok_rows, width)], axis=1
    )
    row_outs, _ = lax.optimization_barrier((row_outs, first_back))
    balanced = lax.all_to_all(row_outs, "seq", 0, 0, tiled=True)
    return (balanced[:, :width], balanced[:, width:], key_grad, value_grad)


def solution(mesh):
    placed = (P("seq", "head"), P("seq", "head"), P("seq", "head"), P("seq", "head"), P(), P())
    return jax.shard_map(
        per_device,
        mesh=mesh,
        in_specs=placed,
        out_specs=(P("seq", "head"), P("seq", "head"), P("seq", "head"), P("seq", "head")),
        check_vma=False,
    )
```

```python
import math

import jax
import jax.numpy as jnp
from jax import lax
from jax.sharding import PartitionSpec as P


masked_value = -1e30
LONGEST = 2048


def doc_index(positions, bounds):
    return jnp.sum((positions[:, None] >= bounds[None, :]).astype(jnp.int32), axis=1)


def per_device(queries, keys, values, grad_out, lengths, send_order):
    shard_count = lax.axis_size("seq")
    my_index = lax.axis_index("seq")
    tok_rows, head_dim = keys.shape
    head_count = queries.shape[1] // head_dim
    score_scale = 1.0 / math.sqrt(head_dim)
    halo = min(shard_count - 1, (LONGEST - 1 + tok_rows - 1) // tok_rows)
    bounds = jnp.cumsum(lengths)

    own_order = lax.dynamic_index_in_dim(send_order, my_index, 0, keepdims=False)
    query_rows = jnp.take(queries, own_order, axis=0)
    query_heads = query_rows.reshape(tok_rows, head_count, head_dim)
    query_pos = my_index * tok_rows + own_order
    query_doc = doc_index(query_pos, bounds)
    grad_rows = lax.all_to_all(grad_out, "seq", 0, 0, tiled=True)
    grad_heads = grad_rows.reshape(tok_rows, head_count, head_dim)

    pair = jnp.concatenate([keys, values], axis=1)
    group = math.isqrt(halo) + 1
    rounds = [
        [(shift, 1) for shift in range(1, min(group, halo + 1))],
        [
            (shift, min(group, halo + 1 - shift))
            for shift in range(group, halo + 1, group)
        ],
    ]
    blocks = [pair]
    for stage in rounds:
        arrived = []
        for shift, count in stage:
            sent = jnp.concatenate(blocks[:count], axis=0)
            got = lax.ppermute(sent, "seq", [(i, i + shift) for i in range(shard_count - shift)])
            arrived.extend(jnp.split(got, count, axis=0))
        blocks.extend(arrived)
    halo_pair = jnp.concatenate(blocks, axis=0)
    key_all = halo_pair[:, :head_dim]
    value_all = halo_pair[:, head_dim:]
    block_ids = jnp.repeat(jnp.arange(halo + 1, dtype=jnp.int32), tok_rows)
    key_pos = (my_index - block_ids) * tok_rows + jnp.tile(
        jnp.arange(tok_rows, dtype=jnp.int32), halo + 1
    )
    key_doc = doc_index(key_pos, bounds)
    allowed = (
        (query_doc[:, None] == key_doc[None, :])
        & (key_pos[None, :] <= query_pos[:, None])
        & (key_pos[None, :] >= 0)
    )[:, None, :]

    products = (
        jnp.einsum("bhd,td->bht", query_heads, key_all, preferred_element_type=jnp.float32)
        * score_scale
    )
    scores = jnp.where(allowed, products, masked_value)
    row_max = jnp.max(scores, axis=2)
    log_total = row_max + jnp.log(jnp.sum(jnp.exp(scores - row_max[:, :, None]), axis=2))
    weights = jnp.where(allowed, jnp.exp(scores - log_total[:, :, None]), 0.0)
    weights_low = weights.astype(jnp.bfloat16)
    attended = jnp.einsum(
        "bht,td->bhd", weights_low, value_all, preferred_element_type=jnp.float32
    )
    attended_low = attended.astype(jnp.bfloat16)
    out_dot = jnp.sum(grad_heads.astype(jnp.float32) * attended_low.astype(jnp.float32), axis=2)
    grad_dots = jnp.einsum(
        "bhd,td->bht", grad_heads, value_all, preferred_element_type=jnp.float32
    )
    score_grads = (weights * (grad_dots - out_dot[:, :, None])).astype(jnp.bfloat16)
    grad_query = (
        jnp.einsum("bht,td->bhd", score_grads, key_all, preferred_element_type=jnp.float32)
        * score_scale
    )
    width = head_count * head_dim
    key_term = (
        jnp.einsum("bht,bhd->td", score_grads, query_heads, preferred_element_type=jnp.float32)
        * score_scale
    )
    value_term = jnp.einsum(
        "bht,bhd->td", weights_low, grad_heads, preferred_element_type=jnp.float32
    )
    terms = jnp.concatenate([key_term, value_term], axis=1)
    parts = list(jnp.split(terms, halo + 1, axis=0))
    for stage in reversed(rounds):
        arrived = []
        for shift, count in stage:
            sent = jnp.concatenate(parts[shift:shift + count], axis=0).astype(jnp.bfloat16)
            got = lax.ppermute(sent, "seq", [(i, i - shift) for i in range(shift, shard_count)])
            arrived.append(jnp.split(got.astype(jnp.float32), count, axis=0))
        for got_parts in arrived:
            for slot, got_part in enumerate(got_parts):
                parts[slot] = parts[slot] + got_part
    total = parts[0]
    key_grad = total[:, :head_dim]
    value_grad = total[:, head_dim:]
    row_outs = jnp.concatenate(
        [attended.reshape(tok_rows, width), grad_query.reshape(tok_rows, width)], axis=1
    )
    balanced = lax.all_to_all(row_outs.astype(jnp.bfloat16), "seq", 0, 0, tiled=True)
    balanced = balanced.astype(jnp.float32)
    return (balanced[:, :width], balanced[:, width:], key_grad, value_grad)


def solution(mesh):
    placed = (P("seq", "head"), P("seq", "head"), P("seq", "head"), P("seq", "head"), P(), P())
    return jax.shard_map(
        per_device,
        mesh=mesh,
        in_specs=placed,
        out_specs=(P("seq", "head"), P("seq", "head"), P("seq", "head"), P("seq", "head")),
        check_vma=False,
    )
```

```python
import math

import jax
import jax.numpy as jnp
from jax import lax
from jax.sharding import PartitionSpec as P


masked_value = -1e30
LONGEST = 2048


def doc_index(positions, bounds):
    return jnp.sum((positions[:, None] >= bounds[None, :]).astype(jnp.int32), axis=1)


def per_device(queries, keys, values, grad_out, lengths, send_order):
    shard_count = lax.axis_size("seq")
    my_index = lax.axis_index("seq")
    tok_rows, head_dim = keys.shape
    head_count = queries.shape[1] // head_dim
    score_scale = 1.0 / math.sqrt(head_dim)
    halo = min(shard_count - 1, (LONGEST - 1 + tok_rows - 1) // tok_rows)
    bounds = jnp.cumsum(lengths)

    own_order = lax.dynamic_index_in_dim(send_order, my_index, 0, keepdims=False)
    query_rows = jnp.take(queries, own_order, axis=0)
    query_heads = query_rows.reshape(tok_rows, head_count, head_dim)
    query_pos = my_index * tok_rows + own_order
    query_doc = doc_index(query_pos, bounds)
    grad_rows = lax.all_to_all(grad_out, "seq", 0, 0, tiled=True)
    grad_heads = grad_rows.reshape(tok_rows, head_count, head_dim)

    pair = jnp.concatenate([keys, values], axis=1)
    group = math.isqrt(halo)
    far = [(shift, group) for shift in range(group, halo + 1 - group + 1, group)]
    covered = group * (len(far) + 1)
    rounds = [
        [(shift, 1) for shift in range(1, group)]
        + [(shift, 1) for shift in range(covered, halo + 1)],
        far,
    ]
    blocks = {0: pair}
    for stage in rounds:
        arrived = {}
        for shift, count in stage:
            sent = jnp.concatenate([blocks[k] for k in range(count)], axis=0)
            got = lax.ppermute(sent, "seq", [(i, i + shift) for i in range(shard_count - shift)])
            for k, piece in enumerate(jnp.split(got, count, axis=0)):
                arrived[shift + k] = piece
        blocks.update(arrived)
    blocks = [blocks[k] for k in range(halo + 1)]
    halo_pair = jnp.concatenate(blocks, axis=0)
    key_all = halo_pair[:, :head_dim]
    value_all = halo_pair[:, head_dim:]
    block_ids = jnp.repeat(jnp.arange(halo + 1, dtype=jnp.int32), tok_rows)
    key_pos = (my_index - block_ids) * tok_rows + jnp.tile(
        jnp.arange(tok_rows, dtype=jnp.int32), halo + 1
    )
    key_doc = doc_index(key_pos, bounds)
    allowed = (
        (query_doc[:, None] == key_doc[None, :])
        & (key_pos[None, :] <= query_pos[:, None])
        & (key_pos[None, :] >= 0)
    )[:, None, :]

    products = (
        jnp.einsum("bhd,td->bht", query_heads, key_all, preferred_element_type=jnp.float32)
        * score_scale
    )
    scores = jnp.where(allowed, products, masked_value)
    row_max = jnp.max(scores, axis=2)
    log_total = row_max + jnp.log(jnp.sum(jnp.exp(scores - row_max[:, :, None]), axis=2))
    weights = jnp.where(allowed, jnp.exp(scores - log_total[:, :, None]), 0.0)
    weights_low = weights.astype(jnp.bfloat16)
    attended = jnp.einsum(
        "bht,td->bhd", weights_low, value_all, preferred_element_type=jnp.float32
    )
    attended_low = attended.astype(jnp.bfloat16)
    out_dot = jnp.sum(grad_heads.astype(jnp.float32) * attended_low.astype(jnp.float32), axis=2)
    grad_dots = jnp.einsum(
        "bhd,td->bht", grad_heads, value_all, preferred_element_type=jnp.float32
    )
    score_grads = (weights * (grad_dots - out_dot[:, :, None])).astype(jnp.bfloat16)
    grad_query = (
        jnp.einsum("bht,td->bhd", score_grads, key_all, preferred_element_type=jnp.float32)
        * score_scale
    )
    width = head_count * head_dim
    key_term = (
        jnp.einsum("bht,bhd->td", score_grads, query_heads, preferred_element_type=jnp.float32)
        * score_scale
    )
    value_term = jnp.einsum(
        "bht,bhd->td", weights_low, grad_heads, preferred_element_type=jnp.float32
    )
    terms = jnp.concatenate([key_term, value_term], axis=1)
    parts = list(jnp.split(terms, halo + 1, axis=0))
    for stage in reversed(rounds):
        arrived = []
        for shift, count in stage:
            sent = jnp.concatenate(parts[shift:shift + count], axis=0).astype(jnp.bfloat16)
            got = lax.ppermute(sent, "seq", [(i, i - shift) for i in range(shift, shard_count)])
            arrived.append(jnp.split(got.astype(jnp.float32), count, axis=0))
        for got_parts in arrived:
            for slot, got_part in enumerate(got_parts):
                parts[slot] = parts[slot] + got_part
    total = parts[0]
    key_grad = total[:, :head_dim]
    value_grad = total[:, head_dim:]
    row_outs = jnp.concatenate(
        [attended.reshape(tok_rows, width), grad_query.reshape(tok_rows, width)], axis=1
    )
    balanced = lax.all_to_all(row_outs.astype(jnp.bfloat16), "seq", 0, 0, tiled=True)
    balanced = balanced.astype(jnp.float32)
    return (balanced[:, :width], balanced[:, width:], key_grad, value_grad)


def solution(mesh):
    placed = (P("seq", "head"), P("seq", "head"), P("seq", "head"), P("seq", "head"), P(), P())
    return jax.shard_map(
        per_device,
        mesh=mesh,
        in_specs=placed,
        out_specs=(P("seq", "head"), P("seq", "head"), P("seq", "head"), P("seq", "head")),
        check_vma=False,
    )
```

```python
import math

import jax
import jax.numpy as jnp
from jax import lax
from jax.sharding import PartitionSpec as P


masked_value = -1e30
LONGEST = 2048


def doc_index(positions, bounds):
    return jnp.sum((positions[:, None] >= bounds[None, :]).astype(jnp.int32), axis=1)


def per_device(queries, keys, values, grad_out, lengths, send_order):
    shard_count = lax.axis_size("seq")
    my_index = lax.axis_index("seq")
    tok_rows, head_dim = keys.shape
    head_count = queries.shape[1] // head_dim
    score_scale = 1.0 / math.sqrt(head_dim)
    halo = min(shard_count - 1, (LONGEST - 1 + tok_rows - 1) // tok_rows)
    bounds = jnp.cumsum(lengths)

    own_order = lax.dynamic_index_in_dim(send_order, my_index, 0, keepdims=False)
    query_rows = jnp.take(queries, own_order, axis=0)
    query_heads = query_rows.reshape(tok_rows, head_count, head_dim)
    query_pos = my_index * tok_rows + own_order
    query_doc = doc_index(query_pos, bounds)
    grad_rows = lax.all_to_all(grad_out, "seq", 0, 0, tiled=True)
    grad_heads = grad_rows.reshape(tok_rows, head_count, head_dim)

    pair = lax.optimization_barrier(jnp.concatenate([keys, values], axis=1))
    group = math.isqrt(halo) + 1
    rounds = [
        [(shift, 1) for shift in range(1, min(group, halo + 1))],
        [
            (shift, min(group, halo + 1 - shift))
            for shift in range(group, halo + 1, group)
        ],
    ]
    blocks = [pair]
    for stage in rounds:
        arrived = []
        for shift, count in stage:
            sent = jnp.concatenate(blocks[:count], axis=0)
            got = lax.ppermute(sent, "seq", [(i, i + shift) for i in range(shard_count - shift)])
            arrived.extend(jnp.split(got, count, axis=0))
        blocks.extend(arrived)
    halo_pair = jnp.concatenate(blocks, axis=0)
    key_all = halo_pair[:, :head_dim]
    value_all = halo_pair[:, head_dim:]
    block_ids = jnp.repeat(jnp.arange(halo + 1, dtype=jnp.int32), tok_rows)
    key_pos = (my_index - block_ids) * tok_rows + jnp.tile(
        jnp.arange(tok_rows, dtype=jnp.int32), halo + 1
    )
    key_doc = doc_index(key_pos, bounds)
    allowed = (
        (query_doc[:, None] == key_doc[None, :])
        & (key_pos[None, :] <= query_pos[:, None])
        & (key_pos[None, :] >= 0)
    )[:, None, :]

    products = (
        jnp.einsum("bhd,td->bht", query_heads, key_all, preferred_element_type=jnp.float32)
        * score_scale
    )
    scores = jnp.where(allowed, products, masked_value)
    row_max = jnp.max(scores, axis=2)
    log_total = row_max + jnp.log(jnp.sum(jnp.exp(scores - row_max[:, :, None]), axis=2))
    weights = jnp.where(allowed, jnp.exp(scores - log_total[:, :, None]), 0.0)
    weights_low = weights.astype(jnp.bfloat16)
    attended = jnp.einsum(
        "bht,td->bhd", weights_low, value_all, preferred_element_type=jnp.float32
    )
    attended_low = attended.astype(jnp.bfloat16)
    out_dot = jnp.sum(grad_heads.astype(jnp.float32) * attended_low.astype(jnp.float32), axis=2)
    grad_dots = jnp.einsum(
        "bhd,td->bht", grad_heads, value_all, preferred_element_type=jnp.float32
    )
    score_grads = (weights * (grad_dots - out_dot[:, :, None])).astype(jnp.bfloat16)
    grad_query = (
        jnp.einsum("bht,td->bhd", score_grads, key_all, preferred_element_type=jnp.float32)
        * score_scale
    )
    width = head_count * head_dim
    key_term = (
        jnp.einsum("bht,bhd->td", score_grads, query_heads, preferred_element_type=jnp.float32)
        * score_scale
    )
    value_term = jnp.einsum(
        "bht,bhd->td", weights_low, grad_heads, preferred_element_type=jnp.float32
    )
    terms = jnp.concatenate([key_term, value_term], axis=1)
    parts = list(jnp.split(terms, halo + 1, axis=0))
    for stage in reversed(rounds):
        arrived = []
        for shift, count in stage:
            sent = jnp.concatenate(parts[shift:shift + count], axis=0).astype(jnp.bfloat16)
            got = lax.ppermute(sent, "seq", [(i, i - shift) for i in range(shift, shard_count)])
            arrived.append(jnp.split(got.astype(jnp.float32), count, axis=0))
        for got_parts in arrived:
            for slot, got_part in enumerate(got_parts):
                parts[slot] = parts[slot] + got_part
    total = parts[0]
    key_grad = total[:, :head_dim]
    value_grad = total[:, head_dim:]
    row_outs = jnp.concatenate(
        [attended.reshape(tok_rows, width), grad_query.reshape(tok_rows, width)], axis=1
    )
    balanced = lax.all_to_all(row_outs.astype(jnp.bfloat16), "seq", 0, 0, tiled=True)
    balanced = balanced.astype(jnp.float32)
    return (balanced[:, :width], balanced[:, width:], key_grad, value_grad)


def solution(mesh):
    placed = (P("seq", "head"), P("seq", "head"), P("seq", "head"), P("seq", "head"), P(), P())
    return jax.shard_map(
        per_device,
        mesh=mesh,
        in_specs=placed,
        out_specs=(P("seq", "head"), P("seq", "head"), P("seq", "head"), P("seq", "head")),
        check_vma=False,
    )
```

```python
import math

import jax
import jax.numpy as jnp
from jax import lax
from jax.sharding import PartitionSpec as P


masked_value = -1e30
LONGEST = 2048


def doc_index(positions, bounds):
    return jnp.sum((positions[:, None] >= bounds[None, :]).astype(jnp.int32), axis=1)


def per_device(queries, keys, values, grad_out, lengths, send_order):
    shard_count = lax.axis_size("seq")
    my_index = lax.axis_index("seq")
    tok_rows, head_dim = keys.shape
    head_count = queries.shape[1] // head_dim
    score_scale = 1.0 / math.sqrt(head_dim)
    halo = min(shard_count - 1, (LONGEST - 1 + tok_rows - 1) // tok_rows)
    bounds = jnp.cumsum(lengths)

    own_order = lax.dynamic_index_in_dim(send_order, my_index, 0, keepdims=False)
    query_rows = jnp.take(queries, own_order, axis=0)
    query_heads = query_rows.reshape(tok_rows, head_count, head_dim)
    query_pos = my_index * tok_rows + own_order
    query_doc = doc_index(query_pos, bounds)
    grad_rows = lax.all_to_all(grad_out, "seq", 0, 0, tiled=True)
    grad_heads = grad_rows.reshape(tok_rows, head_count, head_dim)

    pair = lax.optimization_barrier(jnp.concatenate([keys, values], axis=1))
    group = math.isqrt(halo) + 1
    rounds = [
        [(shift, 1) for shift in range(1, min(group, halo + 1))],
        [
            (shift, min(group, halo + 1 - shift))
            for shift in range(group, halo + 1, group)
        ],
    ]
    blocks = [pair]
    for stage in rounds:
        arrived = []
        for shift, count in stage:
            sent = jnp.concatenate(blocks[:count], axis=0)
            got = lax.ppermute(sent, "seq", [(i, i + shift) for i in range(shard_count - shift)])
            arrived.extend(jnp.split(got, count, axis=0))
        blocks.extend(arrived)
    halo_pair = jnp.concatenate(blocks, axis=0)
    key_all = halo_pair[:, :head_dim]
    value_all = halo_pair[:, head_dim:]
    block_ids = jnp.repeat(jnp.arange(halo + 1, dtype=jnp.int32), tok_rows)
    key_pos = (my_index - block_ids) * tok_rows + jnp.tile(
        jnp.arange(tok_rows, dtype=jnp.int32), halo + 1
    )
    key_doc = doc_index(key_pos, bounds)
    allowed = (
        (query_doc[:, None] == key_doc[None, :])
        & (key_pos[None, :] <= query_pos[:, None])
        & (key_pos[None, :] >= 0)
    )[:, None, :]

    products = (
        jnp.einsum("bhd,td->bht", query_heads, key_all, preferred_element_type=jnp.float32)
        * score_scale
    )
    scores = jnp.where(allowed, products, masked_value)
    row_max = jnp.max(scores, axis=2)
    log_total = row_max + jnp.log(jnp.sum(jnp.exp(scores - row_max[:, :, None]), axis=2))
    weights = jnp.where(allowed, jnp.exp(scores - log_total[:, :, None]), 0.0)
    weights_low = weights.astype(jnp.bfloat16)
    attended = jnp.einsum(
        "bht,td->bhd", weights_low, value_all, preferred_element_type=jnp.float32
    )
    attended_low = attended.astype(jnp.bfloat16)
    out_dot = jnp.sum(grad_heads.astype(jnp.float32) * attended_low.astype(jnp.float32), axis=2)
    grad_dots = jnp.einsum(
        "bhd,td->bht", grad_heads, value_all, preferred_element_type=jnp.float32
    )
    score_grads = (weights * (grad_dots - out_dot[:, :, None])).astype(jnp.bfloat16)
    grad_query = (
        jnp.einsum("bht,td->bhd", score_grads, key_all, preferred_element_type=jnp.float32)
        * score_scale
    )
    width = head_count * head_dim
    key_term = (
        jnp.einsum("bht,bhd->td", score_grads, query_heads, preferred_element_type=jnp.float32)
        * score_scale
    )
    value_term = jnp.einsum(
        "bht,bhd->td", weights_low, grad_heads, preferred_element_type=jnp.float32
    )
    terms = jnp.concatenate([key_term, value_term], axis=1)
    parts = list(jnp.split(terms, halo + 1, axis=0))
    for stage in reversed(rounds):
        arrived = []
        for shift, count in stage:
            sent = jnp.concatenate(parts[shift:shift + count], axis=0).astype(jnp.bfloat16)
            got = lax.ppermute(sent, "seq", [(i, i - shift) for i in range(shift, shard_count)])
            arrived.append(jnp.split(got.astype(jnp.float32), count, axis=0))
        for got_parts in arrived:
            for slot, got_part in enumerate(got_parts):
                parts[slot] = parts[slot] + got_part
    total = parts[0]
    key_grad = total[:, :head_dim]
    value_grad = total[:, head_dim:]
    row_outs = jnp.concatenate(
        [attended.reshape(tok_rows, width), grad_query.reshape(tok_rows, width)], axis=1
    )
    balanced = lax.all_to_all(row_outs.astype(jnp.bfloat16), "seq", 0, 0, tiled=True)
    return (
        balanced[:, :width].astype(jnp.float32),
        balanced[:, width:].astype(jnp.float32),
        key_grad,
        value_grad,
    )


def solution(mesh):
    placed = (P("seq", "head"), P("seq", "head"), P("seq", "head"), P("seq", "head"), P(), P())
    return jax.shard_map(
        per_device,
        mesh=mesh,
        in_specs=placed,
        out_specs=(P("seq", "head"), P("seq", "head"), P("seq", "head"), P("seq", "head")),
        check_vma=False,
    )
```

```python
import math

import jax
import jax.numpy as jnp
from jax import lax
from jax.sharding import PartitionSpec as P


masked_value = -1e30
LONGEST = 2048


def doc_index(positions, bounds):
    return jnp.sum((positions[:, None] >= bounds[None, :]).astype(jnp.int32), axis=1)


def per_device(queries, keys, values, grad_out, lengths, send_order):
    shard_count = lax.axis_size("seq")
    my_index = lax.axis_index("seq")
    tok_rows, head_dim = keys.shape
    head_count = queries.shape[1] // head_dim
    score_scale = 1.0 / math.sqrt(head_dim)
    halo = min(shard_count - 1, (LONGEST - 1 + tok_rows - 1) // tok_rows)
    bounds = jnp.cumsum(lengths)

    own_order = lax.dynamic_index_in_dim(send_order, my_index, 0, keepdims=False)
    query_rows = jnp.take(queries, own_order, axis=0)
    query_heads = query_rows.reshape(tok_rows, head_count, head_dim)
    query_pos = my_index * tok_rows + own_order
    query_doc = doc_index(query_pos, bounds)
    grad_rows = lax.all_to_all(grad_out, "seq", 0, 0, tiled=True)
    grad_heads = grad_rows.reshape(tok_rows, head_count, head_dim)

    pair = lax.optimization_barrier(jnp.concatenate([keys, values], axis=1))
    group = math.isqrt(halo) + 1
    rounds = [
        [(shift, 1) for shift in range(1, min(group, halo + 1))],
        [
            (shift, min(group, halo + 1 - shift))
            for shift in range(group, halo + 1, group)
        ],
    ]
    blocks = [pair]
    for stage in rounds:
        arrived = []
        for shift, count in stage:
            sent = jnp.concatenate(blocks[:count], axis=0)
            got = lax.ppermute(sent, "seq", [(i, i + shift) for i in range(shard_count - shift)])
            arrived.extend(jnp.split(got, count, axis=0))
        blocks.extend(arrived)
    halo_pair = jnp.concatenate(blocks, axis=0)
    key_all = halo_pair[:, :head_dim]
    value_all = halo_pair[:, head_dim:]
    block_ids = jnp.repeat(jnp.arange(halo + 1, dtype=jnp.int32), tok_rows)
    key_pos = (my_index - block_ids) * tok_rows + jnp.tile(
        jnp.arange(tok_rows, dtype=jnp.int32), halo + 1
    )
    key_doc = doc_index(key_pos, bounds)
    allowed = (
        (query_doc[:, None] == key_doc[None, :])
        & (key_pos[None, :] <= query_pos[:, None])
        & (key_pos[None, :] >= 0)
    )[:, None, :]

    products = (
        jnp.einsum("bhd,td->bht", query_heads, key_all, preferred_element_type=jnp.float32)
        * score_scale
    )
    scores = jnp.where(allowed, products, masked_value)
    row_max = jnp.max(scores, axis=2)
    log_total = row_max + jnp.log(jnp.sum(jnp.exp(scores - row_max[:, :, None]), axis=2))
    weights = jnp.where(allowed, jnp.exp(scores - log_total[:, :, None]), 0.0)
    weights_low = weights.astype(jnp.bfloat16)
    attended = jnp.einsum(
        "bht,td->bhd", weights_low, value_all, preferred_element_type=jnp.float32
    )
    attended_low = attended.astype(jnp.bfloat16)
    out_dot = jnp.sum(grad_heads.astype(jnp.float32) * attended_low.astype(jnp.float32), axis=2)
    grad_dots = jnp.einsum(
        "bhd,td->bht", grad_heads, value_all, preferred_element_type=jnp.float32
    )
    score_grads = (weights * (grad_dots - out_dot[:, :, None])).astype(jnp.bfloat16)
    grad_query = (
        jnp.einsum("bht,td->bhd", score_grads, key_all, preferred_element_type=jnp.float32)
        * score_scale
    )
    width = head_count * head_dim
    key_term = (
        jnp.einsum("bht,bhd->td", score_grads, query_heads, preferred_element_type=jnp.float32)
        * score_scale
    )
    value_term = jnp.einsum(
        "bht,bhd->td", weights_low, grad_heads, preferred_element_type=jnp.float32
    )
    terms = jnp.concatenate([key_term, value_term], axis=1)
    parts = list(jnp.split(terms, halo + 1, axis=0))
    for stage in reversed(rounds):
        arrived = []
        for shift, count in stage:
            sent = jnp.concatenate(parts[shift:shift + count], axis=0).astype(jnp.bfloat16)
            got = lax.ppermute(sent, "seq", [(i, i - shift) for i in range(shift, shard_count)])
            arrived.append(jnp.split(got.astype(jnp.float32), count, axis=0))
        for got_parts in arrived:
            for slot, got_part in enumerate(got_parts):
                parts[slot] = parts[slot] + got_part
    total = parts[0]
    key_grad = total[:, :head_dim]
    value_grad = total[:, head_dim:]
    row_outs = jnp.concatenate(
        [attended.reshape(tok_rows, width), grad_query.reshape(tok_rows, width)], axis=1
    )
    row_outs, total = lax.optimization_barrier((row_outs.astype(jnp.bfloat16), total))
    key_grad = total[:, :head_dim]
    value_grad = total[:, head_dim:]
    balanced = lax.all_to_all(row_outs, "seq", 0, 0, tiled=True)
    return (
        balanced[:, :width].astype(jnp.float32),
        balanced[:, width:].astype(jnp.float32),
        key_grad,
        value_grad,
    )


def solution(mesh):
    placed = (P("seq", "head"), P("seq", "head"), P("seq", "head"), P("seq", "head"), P(), P())
    return jax.shard_map(
        per_device,
        mesh=mesh,
        in_specs=placed,
        out_specs=(P("seq", "head"), P("seq", "head"), P("seq", "head"), P("seq", "head")),
        check_vma=False,
    )
```

```python
import math

import jax
import jax.numpy as jnp
from jax import lax
from jax.sharding import PartitionSpec as P


masked_value = -1e30
LONGEST = 2048


def doc_index(positions, bounds):
    return jnp.sum((positions[:, None] >= bounds[None, :]).astype(jnp.int32), axis=1)


def per_device(queries, keys, values, grad_out, lengths, send_order):
    shard_count = lax.axis_size("seq")
    my_index = lax.axis_index("seq")
    tok_rows, head_dim = keys.shape
    head_count = queries.shape[1] // head_dim
    score_scale = 1.0 / math.sqrt(head_dim)
    halo = min(shard_count - 1, (LONGEST - 1 + tok_rows - 1) // tok_rows)
    bounds = jnp.cumsum(lengths)

    own_order = lax.dynamic_index_in_dim(send_order, my_index, 0, keepdims=False)
    query_rows = jnp.take(queries, own_order, axis=0)
    query_heads = query_rows.reshape(tok_rows, head_count, head_dim)
    query_pos = my_index * tok_rows + own_order
    query_doc = doc_index(query_pos, bounds)
    grad_rows = lax.all_to_all(grad_out, "seq", 0, 0, tiled=True)
    grad_heads = grad_rows.reshape(tok_rows, head_count, head_dim)

    pair = lax.optimization_barrier(jnp.concatenate([keys, values], axis=1))
    group = math.isqrt(halo) + 1
    long_shifts = list(range(group, halo + 1, group))
    rounds = [
        [(shift, [0]) for shift in long_shifts],
        [
            (shift, [k for k in [0] + long_shifts if shift + k <= halo])
            for shift in range(1, group)
        ],
    ]
    blocks = {0: pair}
    for stage in rounds:
        arrived = {}
        for shift, offsets in stage:
            sent = jnp.concatenate([blocks[k] for k in offsets], axis=0)
            got = lax.ppermute(sent, "seq", [(i, i + shift) for i in range(shard_count - shift)])
            for k, piece in zip(offsets, jnp.split(got, len(offsets), axis=0)):
                arrived[shift + k] = piece
        blocks.update(arrived)
    blocks = [blocks[k] for k in range(halo + 1)]
    halo_pair = jnp.concatenate(blocks, axis=0)
    key_all = halo_pair[:, :head_dim]
    value_all = halo_pair[:, head_dim:]
    block_ids = jnp.repeat(jnp.arange(halo + 1, dtype=jnp.int32), tok_rows)
    key_pos = (my_index - block_ids) * tok_rows + jnp.tile(
        jnp.arange(tok_rows, dtype=jnp.int32), halo + 1
    )
    key_doc = doc_index(key_pos, bounds)
    allowed = (
        (query_doc[:, None] == key_doc[None, :])
        & (key_pos[None, :] <= query_pos[:, None])
        & (key_pos[None, :] >= 0)
    )[:, None, :]

    products = (
        jnp.einsum("bhd,td->bht", query_heads, key_all, preferred_element_type=jnp.float32)
        * score_scale
    )
    scores = jnp.where(allowed, products, masked_value)
    row_max = jnp.max(scores, axis=2)
    log_total = row_max + jnp.log(jnp.sum(jnp.exp(scores - row_max[:, :, None]), axis=2))
    weights = jnp.where(allowed, jnp.exp(scores - log_total[:, :, None]), 0.0)
    weights_low = weights.astype(jnp.bfloat16)
    attended = jnp.einsum(
        "bht,td->bhd", weights_low, value_all, preferred_element_type=jnp.float32
    )
    attended_low = attended.astype(jnp.bfloat16)
    out_dot = jnp.sum(grad_heads.astype(jnp.float32) * attended_low.astype(jnp.float32), axis=2)
    grad_dots = jnp.einsum(
        "bhd,td->bht", grad_heads, value_all, preferred_element_type=jnp.float32
    )
    score_grads = (weights * (grad_dots - out_dot[:, :, None])).astype(jnp.bfloat16)
    grad_query = (
        jnp.einsum("bht,td->bhd", score_grads, key_all, preferred_element_type=jnp.float32)
        * score_scale
    )
    width = head_count * head_dim
    key_term = (
        jnp.einsum("bht,bhd->td", score_grads, query_heads, preferred_element_type=jnp.float32)
        * score_scale
    )
    value_term = jnp.einsum(
        "bht,bhd->td", weights_low, grad_heads, preferred_element_type=jnp.float32
    )
    terms = jnp.concatenate([key_term, value_term], axis=1)
    parts = list(jnp.split(terms, halo + 1, axis=0))
    for stage in reversed(rounds):
        arrived = []
        for shift, offsets in stage:
            sent = jnp.concatenate([parts[shift + k] for k in offsets], axis=0)
            got = lax.ppermute(
                sent.astype(jnp.bfloat16),
                "seq",
                [(i, i - shift) for i in range(shift, shard_count)],
            )
            arrived.append((offsets, jnp.split(got.astype(jnp.float32), len(offsets), axis=0)))
        for offsets, got_parts in arrived:
            for k, got_part in zip(offsets, got_parts):
                parts[k] = parts[k] + got_part
    total = parts[0]
    key_grad = total[:, :head_dim]
    value_grad = total[:, head_dim:]
    row_outs = jnp.concatenate(
        [attended.reshape(tok_rows, width), grad_query.reshape(tok_rows, width)], axis=1
    )
    balanced = lax.all_to_all(row_outs.astype(jnp.bfloat16), "seq", 0, 0, tiled=True)
    return (
        balanced[:, :width].astype(jnp.float32),
        balanced[:, width:].astype(jnp.float32),
        key_grad,
        value_grad,
    )


def solution(mesh):
    placed = (P("seq", "head"), P("seq", "head"), P("seq", "head"), P("seq", "head"), P(), P())
    return jax.shard_map(
        per_device,
        mesh=mesh,
        in_specs=placed,
        out_specs=(P("seq", "head"), P("seq", "head"), P("seq", "head"), P("seq", "head")),
        check_vma=False,
    )
```

```python
import math

import jax
import jax.numpy as jnp
from jax import lax
from jax.sharding import PartitionSpec as P


masked_value = -1e30
LONGEST = 2048


def doc_index(positions, bounds):
    return jnp.sum((positions[:, None] >= bounds[None, :]).astype(jnp.int32), axis=1)


def per_device(queries, keys, values, grad_out, lengths, send_order):
    shard_count = lax.axis_size("seq")
    my_index = lax.axis_index("seq")
    tok_rows, head_dim = keys.shape
    head_count = queries.shape[1] // head_dim
    score_scale = 1.0 / math.sqrt(head_dim)
    halo = min(shard_count - 1, (LONGEST - 1 + tok_rows - 1) // tok_rows)
    bounds = jnp.cumsum(lengths)

    own_order = lax.dynamic_index_in_dim(send_order, my_index, 0, keepdims=False)
    query_rows = jnp.take(queries, own_order, axis=0)
    query_heads = query_rows.reshape(tok_rows, head_count, head_dim)
    query_pos = my_index * tok_rows + own_order
    query_doc = doc_index(query_pos, bounds)
    grad_rows = lax.all_to_all(grad_out, "seq", 0, 0, tiled=True)
    grad_heads = grad_rows.reshape(tok_rows, head_count, head_dim)

    pair = lax.optimization_barrier(jnp.concatenate([keys, values], axis=1))
    group = math.isqrt(halo) + 1
    rounds = [
        [(shift, 1) for shift in range(1, min(group, halo + 1))],
        [
            (shift, min(group, halo + 1 - shift))
            for shift in range(group, halo + 1, group)
        ],
    ]
    blocks = [pair]
    for stage in rounds:
        arrived = []
        for shift, count in stage:
            sent = jnp.concatenate(blocks[:count], axis=0)
            got = lax.ppermute(sent, "seq", [(i, i + shift) for i in range(shard_count - shift)])
            arrived.extend(jnp.split(got, count, axis=0))
        blocks.extend(arrived)
    halo_pair = jnp.concatenate(blocks, axis=0)
    key_all = halo_pair[:, :head_dim]
    value_all = halo_pair[:, head_dim:]
    block_ids = jnp.repeat(jnp.arange(halo + 1, dtype=jnp.int32), tok_rows)
    key_pos = (my_index - block_ids) * tok_rows + jnp.tile(
        jnp.arange(tok_rows, dtype=jnp.int32), halo + 1
    )
    key_doc = doc_index(key_pos, bounds)
    allowed = (
        (query_doc[:, None] == key_doc[None, :])
        & (key_pos[None, :] <= query_pos[:, None])
        & (key_pos[None, :] >= 0)
    )[:, None, :]

    products = (
        jnp.einsum("bhd,td->bht", query_heads, key_all, preferred_element_type=jnp.float32)
        * score_scale
    )
    scores = jnp.where(allowed, products, masked_value)
    row_max = jnp.max(scores, axis=2)
    log_total = row_max + jnp.log(jnp.sum(jnp.exp(scores - row_max[:, :, None]), axis=2))
    weights = jnp.where(allowed, jnp.exp(scores - log_total[:, :, None]), 0.0)
    weights_low = weights.astype(jnp.bfloat16)
    attended = jnp.einsum(
        "bht,td->bhd", weights_low, value_all, preferred_element_type=jnp.float32
    )
    attended_low = attended.astype(jnp.bfloat16)
    out_dot = jnp.sum(grad_heads.astype(jnp.float32) * attended_low.astype(jnp.float32), axis=2)
    grad_dots = jnp.einsum(
        "bhd,td->bht", grad_heads, value_all, preferred_element_type=jnp.float32
    )
    score_grads = (weights * (grad_dots - out_dot[:, :, None])).astype(jnp.bfloat16)
    grad_query = (
        jnp.einsum("bht,td->bhd", score_grads, key_all, preferred_element_type=jnp.float32)
        * score_scale
    )
    width = head_count * head_dim
    key_term = (
        jnp.einsum("bht,bhd->td", score_grads, query_heads, preferred_element_type=jnp.float32)
        * score_scale
    )
    value_term = jnp.einsum(
        "bht,bhd->td", weights_low, grad_heads, preferred_element_type=jnp.float32
    )
    terms = jnp.concatenate([key_term, value_term], axis=1)
    parts = list(jnp.split(terms, halo + 1, axis=0))
    arrived = []
    for shift in range(halo, 0, -1):
        arrived.append(
            lax.ppermute(
                parts[shift].astype(jnp.bfloat16),
                "seq",
                [(i, i - shift) for i in range(shift, shard_count)],
            )
        )
    for got in arrived:
        parts[0] = parts[0] + got.astype(jnp.float32)
    total = parts[0]
    key_grad = total[:, :head_dim]
    value_grad = total[:, head_dim:]
    row_outs = jnp.concatenate(
        [attended.reshape(tok_rows, width), grad_query.reshape(tok_rows, width)], axis=1
    )
    balanced = lax.all_to_all(row_outs.astype(jnp.bfloat16), "seq", 0, 0, tiled=True)
    return (
        balanced[:, :width].astype(jnp.float32),
        balanced[:, width:].astype(jnp.float32),
        key_grad,
        value_grad,
    )


def solution(mesh):
    placed = (P("seq", "head"), P("seq", "head"), P("seq", "head"), P("seq", "head"), P(), P())
    return jax.shard_map(
        per_device,
        mesh=mesh,
        in_specs=placed,
        out_specs=(P("seq", "head"), P("seq", "head"), P("seq", "head"), P("seq", "head")),
        check_vma=False,
    )
```

```python
import math

import jax
import jax.numpy as jnp
from jax import lax
from jax.sharding import PartitionSpec as P


masked_value = -1e30
LONGEST = 2048


def doc_index(positions, bounds):
    return jnp.sum((positions[:, None] >= bounds[None, :]).astype(jnp.int32), axis=1)


def per_device(queries, keys, values, grad_out, lengths, send_order):
    shard_count = lax.axis_size("seq")
    my_index = lax.axis_index("seq")
    tok_rows, head_dim = keys.shape
    head_count = queries.shape[1] // head_dim
    score_scale = 1.0 / math.sqrt(head_dim)
    halo = min(shard_count - 1, (LONGEST - 1 + tok_rows - 1) // tok_rows)
    bounds = jnp.cumsum(lengths)

    own_order = lax.dynamic_index_in_dim(send_order, my_index, 0, keepdims=False)
    query_rows = jnp.take(queries, own_order, axis=0)
    query_heads = query_rows.reshape(tok_rows, head_count, head_dim)
    query_pos = my_index * tok_rows + own_order
    query_doc = doc_index(query_pos, bounds)
    grad_rows = lax.all_to_all(grad_out, "seq", 0, 0, tiled=True)
    grad_heads = grad_rows.reshape(tok_rows, head_count, head_dim)

    pair, grad_heads = lax.optimization_barrier(
        (jnp.concatenate([keys, values], axis=1), grad_heads)
    )
    group = math.isqrt(halo) + 1
    rounds = [
        [(shift, 1) for shift in range(1, min(group, halo + 1))],
        [
            (shift, min(group, halo + 1 - shift))
            for shift in range(group, halo + 1, group)
        ],
    ]
    blocks = [pair]
    for stage in rounds:
        arrived = []
        for shift, count in stage:
            sent = jnp.concatenate(blocks[:count], axis=0)
            got = lax.ppermute(sent, "seq", [(i, i + shift) for i in range(shard_count - shift)])
            arrived.extend(jnp.split(got, count, axis=0))
        blocks.extend(arrived)
    halo_pair = jnp.concatenate(blocks, axis=0)
    key_all = halo_pair[:, :head_dim]
    value_all = halo_pair[:, head_dim:]
    block_ids = jnp.repeat(jnp.arange(halo + 1, dtype=jnp.int32), tok_rows)
    key_pos = (my_index - block_ids) * tok_rows + jnp.tile(
        jnp.arange(tok_rows, dtype=jnp.int32), halo + 1
    )
    key_doc = doc_index(key_pos, bounds)
    allowed = (
        (query_doc[:, None] == key_doc[None, :])
        & (key_pos[None, :] <= query_pos[:, None])
        & (key_pos[None, :] >= 0)
    )[:, None, :]

    products = (
        jnp.einsum("bhd,td->bht", query_heads, key_all, preferred_element_type=jnp.float32)
        * score_scale
    )
    scores = jnp.where(allowed, products, masked_value)
    row_max = jnp.max(scores, axis=2)
    log_total = row_max + jnp.log(jnp.sum(jnp.exp(scores - row_max[:, :, None]), axis=2))
    weights = jnp.where(allowed, jnp.exp(scores - log_total[:, :, None]), 0.0)
    weights_low = weights.astype(jnp.bfloat16)
    attended = jnp.einsum(
        "bht,td->bhd", weights_low, value_all, preferred_element_type=jnp.float32
    )
    attended_low = attended.astype(jnp.bfloat16)
    out_dot = jnp.sum(grad_heads.astype(jnp.float32) * attended_low.astype(jnp.float32), axis=2)
    grad_dots = jnp.einsum(
        "bhd,td->bht", grad_heads, value_all, preferred_element_type=jnp.float32
    )
    score_grads = (weights * (grad_dots - out_dot[:, :, None])).astype(jnp.bfloat16)
    grad_query = (
        jnp.einsum("bht,td->bhd", score_grads, key_all, preferred_element_type=jnp.float32)
        * score_scale
    )
    width = head_count * head_dim
    key_term = (
        jnp.einsum("bht,bhd->td", score_grads, query_heads, preferred_element_type=jnp.float32)
        * score_scale
    )
    value_term = jnp.einsum(
        "bht,bhd->td", weights_low, grad_heads, preferred_element_type=jnp.float32
    )
    terms = jnp.concatenate([key_term, value_term], axis=1)
    parts = list(jnp.split(terms, halo + 1, axis=0))
    for stage in reversed(rounds):
        arrived = []
        for shift, count in stage:
            sent = jnp.concatenate(parts[shift:shift + count], axis=0).astype(jnp.bfloat16)
            got = lax.ppermute(sent, "seq", [(i, i - shift) for i in range(shift, shard_count)])
            arrived.append(jnp.split(got.astype(jnp.float32), count, axis=0))
        for got_parts in arrived:
            for slot, got_part in enumerate(got_parts):
                parts[slot] = parts[slot] + got_part
    total = parts[0]
    key_grad = total[:, :head_dim]
    value_grad = total[:, head_dim:]
    row_outs = jnp.concatenate(
        [attended.reshape(tok_rows, width), grad_query.reshape(tok_rows, width)], axis=1
    )
    balanced = lax.all_to_all(row_outs.astype(jnp.bfloat16), "seq", 0, 0, tiled=True)
    return (
        balanced[:, :width].astype(jnp.float32),
        balanced[:, width:].astype(jnp.float32),
        key_grad,
        value_grad,
    )


def solution(mesh):
    placed = (P("seq", "head"), P("seq", "head"), P("seq", "head"), P("seq", "head"), P(), P())
    return jax.shard_map(
        per_device,
        mesh=mesh,
        in_specs=placed,
        out_specs=(P("seq", "head"), P("seq", "head"), P("seq", "head"), P("seq", "head")),
        check_vma=False,
    )
```

```python
import math

import jax
import jax.numpy as jnp
from jax import lax
from jax.sharding import PartitionSpec as P


masked_value = -1e30
LONGEST = 2048


def doc_index(positions, bounds):
    return jnp.sum((positions[:, None] >= bounds[None, :]).astype(jnp.int32), axis=1)


def per_device(queries, keys, values, grad_out, lengths, send_order):
    shard_count = lax.axis_size("seq")
    my_index = lax.axis_index("seq")
    tok_rows, head_dim = keys.shape
    head_count = queries.shape[1] // head_dim
    score_scale = 1.0 / math.sqrt(head_dim)
    halo = min(shard_count - 1, (LONGEST - 1 + tok_rows - 1) // tok_rows)
    bounds = jnp.cumsum(lengths)

    own_order = lax.dynamic_index_in_dim(send_order, my_index, 0, keepdims=False)
    query_rows = jnp.take(queries, own_order, axis=0)
    query_heads = query_rows.reshape(tok_rows, head_count, head_dim)
    query_pos = my_index * tok_rows + own_order
    query_doc = doc_index(query_pos, bounds)
    grad_rows = lax.all_to_all(grad_out, "seq", 0, 0, tiled=True)
    grad_heads = grad_rows.reshape(tok_rows, head_count, head_dim)

    pair = lax.optimization_barrier(jnp.concatenate([keys, values], axis=1))
    group = math.isqrt(halo) + 1
    rounds = [
        [(shift, 1) for shift in range(1, min(group, halo + 1))],
        [
            (shift, min(group, halo + 1 - shift))
            for shift in range(group, halo + 1, group)
        ],
    ]
    blocks = [pair]
    for stage in rounds:
        arrived = []
        for shift, count in stage:
            sent = jnp.concatenate(blocks[:count], axis=0)
            got = lax.ppermute(sent, "seq", [(i, i + shift) for i in range(shard_count - shift)])
            arrived.extend(jnp.split(got, count, axis=0))
        blocks.extend(arrived)
    halo_pair = jnp.concatenate(blocks, axis=0)
    key_all = halo_pair[:, :head_dim]
    value_all = halo_pair[:, head_dim:]
    block_ids = jnp.repeat(jnp.arange(halo + 1, dtype=jnp.int32), tok_rows)
    key_pos = (my_index - block_ids) * tok_rows + jnp.tile(
        jnp.arange(tok_rows, dtype=jnp.int32), halo + 1
    )
    key_doc = doc_index(key_pos, bounds)
    allowed = (
        (query_doc[:, None] == key_doc[None, :])
        & (key_pos[None, :] <= query_pos[:, None])
        & (key_pos[None, :] >= 0)
    )[:, None, :]

    products = (
        jnp.einsum("bhd,td->bht", query_heads, key_all, preferred_element_type=jnp.float32)
        * score_scale
    )
    scores = jnp.where(allowed, products, masked_value)
    row_max = jnp.max(scores, axis=2)
    log_total = row_max + jnp.log(jnp.sum(jnp.exp(scores - row_max[:, :, None]), axis=2))
    weights = jnp.where(allowed, jnp.exp(scores - log_total[:, :, None]), 0.0)
    weights_low = weights.astype(jnp.bfloat16)
    attended = jnp.einsum(
        "bht,td->bhd", weights_low, value_all, preferred_element_type=jnp.float32
    )
    attended_low = attended.astype(jnp.bfloat16)
    out_dot = jnp.sum(grad_heads.astype(jnp.float32) * attended_low.astype(jnp.float32), axis=2)
    grad_dots = jnp.einsum(
        "bhd,td->bht", grad_heads, value_all, preferred_element_type=jnp.float32
    )
    score_grads = (weights * (grad_dots - out_dot[:, :, None])).astype(jnp.bfloat16)
    grad_query = (
        jnp.einsum("bht,td->bhd", score_grads, key_all, preferred_element_type=jnp.float32)
        * score_scale
    )
    width = head_count * head_dim
    key_term = (
        jnp.einsum("bht,bhd->td", score_grads, query_heads, preferred_element_type=jnp.float32)
        * score_scale
    )
    value_term = jnp.einsum(
        "bht,bhd->td", weights_low, grad_heads, preferred_element_type=jnp.float32
    )
    terms = jnp.concatenate([key_term, value_term], axis=1)
    parts = list(jnp.split(terms, halo + 1, axis=0))
    for stage in reversed(rounds):
        arrived = []
        for shift, count in stage:
            sent = jnp.concatenate(parts[shift:shift + count], axis=0).astype(jnp.bfloat16)
            got = lax.ppermute(sent, "seq", [(i, i - shift) for i in range(shift, shard_count)])
            arrived.append(jnp.split(got, count, axis=0))
        for got_parts in arrived:
            for slot, got_part in enumerate(got_parts):
                parts[slot] = parts[slot] + got_part.astype(jnp.float32)
    total = parts[0]
    key_grad = total[:, :head_dim]
    value_grad = total[:, head_dim:]
    row_outs = jnp.concatenate(
        [attended.reshape(tok_rows, width), grad_query.reshape(tok_rows, width)], axis=1
    )
    balanced = lax.all_to_all(row_outs.astype(jnp.bfloat16), "seq", 0, 0, tiled=True)
    return (
        balanced[:, :width].astype(jnp.float32),
        balanced[:, width:].astype(jnp.float32),
        key_grad,
        value_grad,
    )


def solution(mesh):
    placed = (P("seq", "head"), P("seq", "head"), P("seq", "head"), P("seq", "head"), P(), P())
    return jax.shard_map(
        per_device,
        mesh=mesh,
        in_specs=placed,
        out_specs=(P("seq", "head"), P("seq", "head"), P("seq", "head"), P("seq", "head")),
        check_vma=False,
    )
```

```python
import math

import jax
import jax.numpy as jnp
from jax import lax
from jax.sharding import PartitionSpec as P


masked_value = -1e30
LONGEST = 2048


def doc_index(positions, bounds):
    return jnp.sum((positions[:, None] >= bounds[None, :]).astype(jnp.int32), axis=1)


def per_device(queries, keys, values, grad_out, lengths, send_order):
    shard_count = lax.axis_size("seq")
    my_index = lax.axis_index("seq")
    tok_rows, head_dim = keys.shape
    head_count = queries.shape[1] // head_dim
    score_scale = 1.0 / math.sqrt(head_dim)
    halo = min(shard_count - 1, (LONGEST - 1 + tok_rows - 1) // tok_rows)
    bounds = jnp.cumsum(lengths)

    own_order = lax.dynamic_index_in_dim(send_order, my_index, 0, keepdims=False)
    query_rows = jnp.take(queries, own_order, axis=0)
    query_heads = query_rows.reshape(tok_rows, head_count, head_dim)
    query_pos = my_index * tok_rows + own_order
    query_doc = doc_index(query_pos, bounds)
    grad_rows = lax.all_to_all(grad_out, "seq", 0, 0, tiled=True)
    grad_heads = grad_rows.reshape(tok_rows, head_count, head_dim)

    pair = lax.optimization_barrier(jnp.concatenate([keys, values], axis=1))
    group = math.isqrt(halo) + 1
    rounds = [
        [(shift, 1) for shift in range(1, min(group, halo + 1))],
        [
            (shift, min(group, halo + 1 - shift))
            for shift in range(group, halo + 1, group)
        ],
    ]
    blocks = [pair]
    for stage in rounds:
        arrived = []
        for shift, count in stage:
            sent = jnp.concatenate(blocks[:count], axis=0)
            got = lax.ppermute(sent, "seq", [(i, i + shift) for i in range(shard_count - shift)])
            arrived.extend(jnp.split(got, count, axis=0))
        blocks.extend(arrived)
    halo_pair = jnp.concatenate(blocks, axis=0)
    key_all = halo_pair[:, :head_dim]
    value_all = halo_pair[:, head_dim:]
    block_ids = jnp.repeat(jnp.arange(halo + 1, dtype=jnp.int32), tok_rows)
    key_pos = (my_index - block_ids) * tok_rows + jnp.tile(
        jnp.arange(tok_rows, dtype=jnp.int32), halo + 1
    )
    key_doc = doc_index(key_pos, bounds)
    allowed = (
        (query_doc[:, None] == key_doc[None, :])
        & (key_pos[None, :] <= query_pos[:, None])
        & (key_pos[None, :] >= 0)
    )[:, None, :]

    products = (
        jnp.einsum("bhd,td->bht", query_heads, key_all, preferred_element_type=jnp.float32)
        * score_scale
    )
    scores = jnp.where(allowed, products, masked_value)
    row_max = jnp.max(scores, axis=2)
    log_total = row_max + jnp.log(jnp.sum(jnp.exp(scores - row_max[:, :, None]), axis=2))
    weights = jnp.where(allowed, jnp.exp(scores - log_total[:, :, None]), 0.0)
    weights_low = weights.astype(jnp.bfloat16)
    attended = jnp.einsum(
        "bht,td->bhd", weights_low, value_all, preferred_element_type=jnp.float32
    )
    attended_low = attended.astype(jnp.bfloat16)
    out_dot = jnp.sum(grad_heads.astype(jnp.float32) * attended_low.astype(jnp.float32), axis=2)
    grad_dots = jnp.einsum(
        "bhd,td->bht", grad_heads, value_all, preferred_element_type=jnp.float32
    )
    score_grads = (weights * (grad_dots - out_dot[:, :, None])).astype(jnp.bfloat16)
    width = head_count * head_dim
    key_term = (
        jnp.einsum("bht,bhd->td", score_grads, query_heads, preferred_element_type=jnp.float32)
        * score_scale
    )
    value_term = jnp.einsum(
        "bht,bhd->td", weights_low, grad_heads, preferred_element_type=jnp.float32
    )
    terms = jnp.concatenate([key_term, value_term], axis=1)
    query_grads, _ = lax.optimization_barrier((score_grads, terms))
    grad_query = (
        jnp.einsum("bht,td->bhd", query_grads, key_all, preferred_element_type=jnp.float32)
        * score_scale
    )
    parts = list(jnp.split(terms, halo + 1, axis=0))
    for stage in reversed(rounds):
        arrived = []
        for shift, count in stage:
            sent = jnp.concatenate(parts[shift:shift + count], axis=0).astype(jnp.bfloat16)
            got = lax.ppermute(sent, "seq", [(i, i - shift) for i in range(shift, shard_count)])
            arrived.append(jnp.split(got, count, axis=0))
        for got_parts in arrived:
            for slot, got_part in enumerate(got_parts):
                parts[slot] = parts[slot] + got_part.astype(jnp.float32)
    total = parts[0]
    key_grad = total[:, :head_dim]
    value_grad = total[:, head_dim:]
    row_outs = jnp.concatenate(
        [attended.reshape(tok_rows, width), grad_query.reshape(tok_rows, width)], axis=1
    )
    balanced = lax.all_to_all(row_outs.astype(jnp.bfloat16), "seq", 0, 0, tiled=True)
    return (
        balanced[:, :width].astype(jnp.float32),
        balanced[:, width:].astype(jnp.float32),
        key_grad,
        value_grad,
    )


def solution(mesh):
    placed = (P("seq", "head"), P("seq", "head"), P("seq", "head"), P("seq", "head"), P(), P())
    return jax.shard_map(
        per_device,
        mesh=mesh,
        in_specs=placed,
        out_specs=(P("seq", "head"), P("seq", "head"), P("seq", "head"), P("seq", "head")),
        check_vma=False,
    )
```
